256 devices in a mesh: wave: 32 (over z, x), tile: 8 (over y, core).
Axes of the slice: x: 4, y: 4, z: 8, core: 2. Of those that a mesh axis runs over, the one named last changes fastest.
Arguments:
- scene: float32 [32, 2048, 1024], P('wave', 'tile'), may hold values from -6 to 6
- bank: float32 [32, 16, 8, 128, 128], P('wave', 'tile'), may hold values from -0.046875 to 0.046875
- psf_index: int32 [16, 8, 4], P('tile'), may hold values from 0 to 127, as said below
- psf_weight: int32 [16, 8, 4], P('tile'), may hold values from 1 to 32768
- response: float32 [3, 32], replicated, may hold values from -1 to 1
Outputs:
- colour: float32 [3, 2048, 1024], P(None, ('tile', 'wave'))
The draws below stay inside these ranges and needn't reach their ends.
Inputs may be any that keep to these rules, and one draw needn't show every extreme that they name: Entry k of tile (r, c) names the field point (psf_index // 8, psf_index % 8), which lies at most one tile row and at most one tile column from (r, c); entry 0 names (r, c) itself.
All inputs are finite; a program needn't handle non-finite values.
Results may differ from the reference program's by a relative error of at most 0.0001.
Values sent between devices are 32-bit elements; how exact they have to be, the bound alone decides.
No kernel may reach another device: no remote copies, remote signals or barrier semaphores. Data moves between devices by JAX's collectives and lax.ppermute only.
A program may use at most 64 MiB of HBM per device.

```python
import jax
import jax.numpy as jnp
from jax import lax

P_SIZE = 128
WAVES = 32
K = 4
GC = 8
GR = 16
H = 2048
W = 1024


def draw_psf_index(key, part):
    key_rows, key_cols = jax.random.split(key)
    row_ids = lax.iota(jnp.int32, GR)[:, None, None]
    col_ids = lax.iota(jnp.int32, GC)[None, :, None]
    first_entry = (lax.iota(jnp.int32, K) == 0)[None, None, :]
    row_step = jax.random.randint(key_rows, (GR, GC, K), -1, 2)
    col_step = jax.random.randint(key_cols, (GR, GC, K), -1, 2)
    row_step = jnp.where(first_entry, 0, row_step)
    col_step = jnp.where(first_entry, 0, col_step)
    row_pick = jnp.clip(row_ids + row_step, 0, GR - 1)
    col_pick = jnp.clip(col_ids + col_step, 0, GC - 1)
    return (row_pick * GC + col_pick).astype(jnp.int32)


def set_ends(result, own_key, smallest, top_value):
    place = [jax.random.randint(jax.random.fold_in(own_key, axis), (), 0, length) for axis, length in enumerate(result.shape)]
    longest = result.shape.index(max(result.shape))
    neighbour = place[:longest] + [(place[longest] + 1) % result.shape[longest]] + place[longest + 1:]
    return result.at[tuple(place)].set(smallest).at[tuple(neighbour)].set(top_value)


def levels(stream_key, extent, cuts, least, high):
    loudness = 1.0
    for dim, blocks in cuts:
        draws = jax.random.uniform(jax.random.fold_in(jax.random.fold_in(stream_key, 6), dim), (blocks,), jnp.float32, least / len(cuts), high / len(cuts))
        loudness = loudness * jnp.repeat(jnp.exp(draws), extent[dim] // blocks).reshape((-1,) + (1,) * (len(extent) - 1 - dim))
    return loudness


def normal_values(key, dims, spread, reach, shards=(), dtype=jnp.bfloat16):
    result = spread * jax.random.normal(key, dims, jnp.float32)
    if shards:
        result = result * levels(key, dims, shards, -0.22, 0.18)
    return jnp.clip(result, -reach, reach).astype(dtype)


def setup_inputs(seed: int = 0) -> dict:
    key_list = jax.random.split(jax.random.key(seed), 6)
    return {
        "scene": normal_values(key_list[0], (WAVES, H, W), 1.0, 6.0, ((0, 32), (1, 8)), jnp.float32),
        "bank": normal_values(key_list[1], (WAVES, GR, GC, P_SIZE, P_SIZE), (P_SIZE * P_SIZE) ** -0.5, 0.046875, ((0, 32), (1, 8)), jnp.float32),
        "psf_index": draw_psf_index(jax.random.fold_in(key_list[5], 71), 0),
        "psf_weight": set_ends(jax.random.randint(key_list[3], (GR, GC, K), 1, 32769), jax.random.fold_in(key_list[3], 1), 1, 32768).astype(jnp.int32),
        "response": normal_values(key_list[4], (3, WAVES), WAVES ** -0.5, 1.0, (), jnp.float32),
    }


def blur_wave(scene_plane, bank_plane, psf_index, psf_weight):
    tile_rows, tile_cols, side = bank_plane.shape[0], bank_plane.shape[1], bank_plane.shape[-1]
    length = 2 * side
    margin = side // 2
    flat_bank = bank_plane.reshape(tile_rows * tile_cols, side, side)
    fraction = psf_weight.astype(jnp.float32) / 65536.0
    psf_set = jnp.einsum('rck,rckab->rcab', fraction, flat_bank[psf_index], precision=lax.Precision.HIGHEST)
    tile_set = scene_plane.reshape(tile_rows, side, tile_cols, side).transpose(0, 2, 1, 3)
    scene_spec = jnp.fft.rfft2(tile_set, s=(length, length))
    psf_spec = jnp.fft.rfft2(psf_set, s=(length, length))
    circular = jnp.fft.irfft2(scene_spec * psf_spec, s=(length, length))
    left_half = jnp.pad(circular[..., :side], ((0, 0), (0, 1), (0, 0), (0, 0)))
    right_half = jnp.pad(circular[..., side:], ((0, 0), (1, 0), (0, 0), (0, 0)))
    columns = (left_half + right_half).transpose(0, 2, 1, 3).reshape(tile_rows, length, (tile_cols + 1) * side)
    columns = columns[:, :, margin:margin + tile_cols * side]
    top_half = jnp.pad(columns[:, :side], ((0, 1), (0, 0), (0, 0)))
    bottom_half = jnp.pad(columns[:, side:], ((1, 0), (0, 0), (0, 0)))
    summed = (top_half + bottom_half).reshape((tile_rows + 1) * side, tile_cols * side)
    return summed[margin:margin + tile_rows * side]


def reference(scene, bank, psf_index, psf_weight, response):
    def accumulate(total, inputs):
        scene_plane, bank_plane, weights_now = inputs
        blurred = blur_wave(scene_plane, bank_plane, psf_index, psf_weight)
        return total + weights_now[:, None, None] * blurred[None], None

    start = jnp.zeros((3, scene.shape[1], scene.shape[2]), jnp.float32)
    colour, unused = lax.scan(accumulate, start, (scene, bank, response.T))
    return colour
```

```python
import math

import jax
import jax.numpy as jnp
from jax import lax
from jax.sharding import PartitionSpec as P

highest = lax.Precision.HIGHEST


def with_halo(cells, sides, width):
    for axis, dim in sides:
        count = lax.axis_size(axis)
        ends = count - 1
        head = lax.slice_in_dim(cells, 0, width, axis=dim)
        tail = lax.slice_in_dim(cells, cells.shape[dim] - width, cells.shape[dim], axis=dim)
        cells = jnp.concatenate(
            [
                lax.ppermute(tail, axis, [(i, (i + 1) % count) for i in range(ends)]),
                cells,
                lax.ppermute(head, axis, [((i + 1) % count, i) for i in range(ends)]),
            ],
            axis=dim,
        )
    return cells


def from_behind(shard, axis, by):
    size = lax.axis_size(axis)
    pairs = [(i, i + by) for i in range(size) if 0 <= i + by < size]
    return lax.ppermute(shard, axis, pairs)


def dft_tables(length):
    counter = lax.iota(jnp.int32, length)
    products = counter[:, None] * counter[None, :] % length
    angles = products.astype(jnp.float32) * (2.0 * math.pi / length)
    return (jnp.cos(angles), jnp.sin(angles))


def forward(blocks, cosine, sine):
    side = blocks.shape[-1]
    cos_top = cosine[:side, :]
    sin_top = sine[:side, :]
    row_real = jnp.einsum("ak,tab->tkb", cos_top, blocks, precision=highest)
    row_imag = -jnp.einsum("ak,tab->tkb", sin_top, blocks, precision=highest)
    spec_real = jnp.einsum("tkb,bl->tkl", row_real, cos_top, precision=highest) + jnp.einsum(
        "tkb,bl->tkl", row_imag, sin_top, precision=highest
    )
    spec_imag = jnp.einsum("tkb,bl->tkl", row_imag, cos_top, precision=highest) - jnp.einsum(
        "tkb,bl->tkl", row_real, sin_top, precision=highest
    )
    return (spec_real, spec_imag)


def inverse(prod_real, prod_imag, cosine, sine):
    length = cosine.shape[0]
    part_real = jnp.einsum("mk,tkl->tml", cosine, prod_real, precision=highest) - jnp.einsum(
        "mk,tkl->tml", sine, prod_imag, precision=highest
    )
    part_imag = jnp.einsum("mk,tkl->tml", sine, prod_real, precision=highest) + jnp.einsum(
        "mk,tkl->tml", cosine, prod_imag, precision=highest
    )
    result = jnp.einsum("tml,ln->tmn", part_real, cosine, precision=highest) - jnp.einsum(
        "tml,ln->tmn", part_imag, sine, precision=highest
    )
    return result / float(length * length)


def blur_row(scene_row, psf_row, cosine, sine):
    tile_cols, side = (psf_row.shape[0], psf_row.shape[-1])
    length = 2 * side
    margin = side // 2
    tile_set = scene_row.reshape(side, tile_cols, side).transpose(1, 0, 2)
    scene_real, scene_imag = forward(tile_set, cosine, sine)
    psf_real, psf_imag = forward(psf_row, cosine, sine)
    prod_real = scene_real * psf_real - scene_imag * psf_imag
    prod_imag = scene_real * psf_imag + scene_imag * psf_real
    circular = inverse(prod_real, prod_imag, cosine, sine)
    left_half = jnp.pad(circular[:, :, :side], ((0, 1), (0, 0), (0, 0)))
    right_half = jnp.pad(circular[:, :, side:], ((1, 0), (0, 0), (0, 0)))
    columns = (left_half + right_half).transpose(1, 0, 2).reshape(length, (tile_cols + 1) * side)
    return columns[:, margin : margin + tile_cols * side]


def blur_wave(scene_plane, extended_plane, mixing, cosine, sine):
    slots, tile_cols, side = (
        extended_plane.shape[0] * extended_plane.shape[1],
        extended_plane.shape[1],
        extended_plane.shape[-1],
    )
    tile_rows = extended_plane.shape[0] - 2
    width = scene_plane.shape[1]
    psf_set = jnp.dot(mixing, extended_plane.reshape(slots, side * side), precision=highest)
    psf_set = psf_set.reshape(tile_rows, tile_cols, side, side)
    scene_rows = scene_plane.reshape(tile_rows, side, width)

    def one_row(inputs):
        return blur_row(inputs[0], inputs[1], cosine, sine)

    rows_out = lax.map(one_row, (scene_rows, psf_set))
    top_half = jnp.pad(rows_out[:, :side], ((0, 1), (0, 0), (0, 0)))
    bottom_half = jnp.pad(rows_out[:, side:], ((1, 0), (0, 0), (0, 0)))
    return (top_half + bottom_half).reshape((tile_rows + 1) * side, width)


def per_device(scene, bank, psf_index, psf_weight, response):
    wave_count, tile_rows, tile_cols, side = (
        bank.shape[0],
        bank.shape[1],
        bank.shape[2],
        bank.shape[3],
    )
    entries = psf_index.shape[-1]
    margin = side // 2
    strip = tile_rows * side
    extended = with_halo(bank, (("tile", 1),), 1)
    first_slot = (lax.axis_index("tile") * tile_rows - 1) * tile_cols
    local_slot = psf_index.reshape(tile_rows * tile_cols, entries) - first_slot
    slot_ids = lax.iota(jnp.int32, (tile_rows + 2) * tile_cols)
    fraction = psf_weight.reshape(tile_rows * tile_cols, entries).astype(jnp.float32) / 65536.0
    mixing = jnp.sum(
        jnp.where(local_slot[:, :, None] == slot_ids[None, None, :], fraction[:, :, None], 0.0),
        axis=1,
    )
    cosine, sine = dft_tables(2 * side)

    def one_wave(inputs):
        return blur_wave(inputs[0], inputs[1], mixing, cosine, sine)

    summed = lax.map(one_wave, (scene, extended))
    from_above = from_behind(summed[:, strip + margin :], "tile", 1)
    from_below = from_behind(summed[:, :margin], "tile", -1)
    blurred = summed[:, margin : margin + strip]
    blurred = blurred.at[:, :margin].add(from_above)
    blurred = blurred.at[:, strip - margin :].add(from_below)
    groups = lax.axis_size("wave")
    width = blurred.shape[-1]
    pieces = blurred.reshape(wave_count, groups, strip // groups, width)
    gathered = lax.all_to_all(pieces, "wave", 1, 1, tiled=True)
    channels = response.shape[0]
    spectral = response.reshape(channels, groups, wave_count)
    colour = jnp.einsum("csi,isrx->crx", spectral, gathered, precision=highest)
    return colour


def solution(mesh):
    in_specs = (
        P("wave", "tile", None),
        P("wave", "tile", None, None, None),
        P("tile", None, None),
        P("tile", None, None),
        P(),
    )
    out_specs = P(None, ("tile", "wave"), None)
    return jax.shard_map(
        per_device, mesh=mesh, in_specs=in_specs, out_specs=out_specs, check_vma=False
    )
```

```python
import math

import jax
import jax.numpy as jnp
from jax import lax
from jax.sharding import PartitionSpec as P

highest = lax.Precision.HIGHEST
high = lax.Precision.HIGH


def with_halo(cells, sides, width):
    for axis, dim in sides:
        count = lax.axis_size(axis)
        ends = count - 1
        head = lax.slice_in_dim(cells, 0, width, axis=dim)
        tail = lax.slice_in_dim(cells, cells.shape[dim] - width, cells.shape[dim], axis=dim)
        cells = jnp.concatenate(
            [
                lax.ppermute(tail, axis, [(i, (i + 1) % count) for i in range(ends)]),
                cells,
                lax.ppermute(head, axis, [((i + 1) % count, i) for i in range(ends)]),
            ],
            axis=dim,
        )
    return cells


def from_behind(shard, axis, by):
    size = lax.axis_size(axis)
    pairs = [(i, i + by) for i in range(size) if 0 <= i + by < size]
    return lax.ppermute(shard, axis, pairs)


def angle_table(rows, cols, length):
    products = lax.iota(jnp.int32, rows)[:, None] * lax.iota(jnp.int32, cols)[None, :] % length
    angles = products.astype(jnp.float32) * (2.0 * math.pi / length)
    return jnp.cos(angles), jnp.sin(angles)


def dft_tables(side):
    length = 2 * side
    half = side
    cos_in, sin_in = angle_table(side, half, length)
    alternating = jnp.where(lax.iota(jnp.int32, side) % 2 == 0, 1.0, -1.0).astype(jnp.float32)
    first = jnp.concatenate([cos_in, (-sin_in).at[:, 0].set(alternating)], axis=1)
    cos_top, sin_top = angle_table(side, length, length)
    rows_fwd = jnp.concatenate([cos_top, sin_top], axis=1)
    cos_full, sin_full = angle_table(length, length, length)
    rows_inv = jnp.concatenate([cos_full, sin_full], axis=1)
    cos_out, sin_out = angle_table(half, length, length)
    every = jnp.where(lax.iota(jnp.int32, length) % 2 == 0, 1.0, -1.0).astype(jnp.float32)
    cos_out = (2.0 * cos_out).at[0].set(1.0)
    sin_out = (-2.0 * sin_out).at[0].set(every)
    last = jnp.concatenate([cos_out, sin_out], axis=0) / float(length * length)
    return first, rows_fwd, rows_inv, last


def forward(blocks, first, rows_fwd):
    half = first.shape[1] // 2
    length = rows_fwd.shape[1] // 2
    packed = jnp.einsum("tab,bj->taj", blocks, first, precision=highest)
    both = jnp.einsum("ak,taj->tkj", rows_fwd, packed, precision=highest)
    by_cos, by_sin = both[:, :length], both[:, length:]
    spec_real = by_cos[..., :half] + by_sin[..., half:]
    spec_imag = by_cos[..., half:] - by_sin[..., :half]
    return spec_real, spec_imag


def reverse(values):
    return jnp.roll(jnp.flip(values, axis=-1), 1, axis=-1)


def split_packed(real, imag):
    real_rev, imag_rev = reverse(real), reverse(imag)
    low = (0.5 * (real + real_rev), 0.5 * (imag - imag_rev))
    top = (0.5 * (imag + imag_rev), -0.5 * (real - real_rev))
    return low, top


def times(a, b):
    return (a[0] * b[0] - a[1] * b[1], a[0] * b[1] + a[1] * b[0])


def product(scene_spec, psf_spec):
    prod_real, prod_imag = times(scene_spec, psf_spec)
    scene_low, scene_top = split_packed(scene_spec[0][..., 0], scene_spec[1][..., 0])
    psf_low, psf_top = split_packed(psf_spec[0][..., 0], psf_spec[1][..., 0])
    low = times(scene_low, psf_low)
    top = times(scene_top, psf_top)
    prod_real = prod_real.at[..., 0].set(low[0] - top[1])
    prod_imag = prod_imag.at[..., 0].set(low[1] + top[0])
    return prod_real, prod_imag


def inverse(prod_real, prod_imag, rows_inv, last):
    half = prod_real.shape[-1]
    length = rows_inv.shape[0]
    stacked = jnp.concatenate([prod_real, prod_imag], axis=-1)
    both = jnp.einsum("km,tkj->tmj", rows_inv, stacked, precision=high)
    by_cos, by_sin = both[:, :length], both[:, length:]
    part_real = by_cos[..., :half] - by_sin[..., half:]
    part_imag = by_sin[..., :half] + by_cos[..., half:]
    packed = jnp.concatenate([part_real, part_imag], axis=-1)
    return jnp.einsum("tmj,jn->tmn", packed, last, precision=high)


def blur_wave(scene_plane, extended_plane, mixing, tables):
    first, rows_fwd, rows_inv, last = tables
    slots, tile_cols, side = (
        extended_plane.shape[0] * extended_plane.shape[1],
        extended_plane.shape[1],
        extended_plane.shape[-1],
    )
    tile_rows = extended_plane.shape[0] - 2
    tiles = tile_rows * tile_cols
    width = scene_plane.shape[1]
    margin = side // 2
    psf_set = jnp.dot(mixing, extended_plane.reshape(slots, side * side), precision=highest)
    psf_set = psf_set.reshape(tiles, side, side)
    tile_set = (
        scene_plane.reshape(tile_rows, side, tile_cols, side)
        .transpose(0, 2, 1, 3)
        .reshape(tiles, side, side)
    )
    spec_real, spec_imag = forward(jnp.concatenate([tile_set, psf_set]), first, rows_fwd)
    prod_real, prod_imag = product(
        (spec_real[:tiles], spec_imag[:tiles]), (spec_real[tiles:], spec_imag[tiles:])
    )
    circular = inverse(prod_real, prod_imag, rows_inv, last)
    circular = circular.reshape(tile_rows, tile_cols, 2 * side, 2 * side)
    left_half = jnp.pad(circular[..., :side], ((0, 0), (0, 1), (0, 0), (0, 0)))
    right_half = jnp.pad(circular[..., side:], ((0, 0), (1, 0), (0, 0), (0, 0)))
    columns = (left_half + right_half).transpose(0, 2, 1, 3)
    columns = columns.reshape(tile_rows, 2 * side, (tile_cols + 1) * side)
    columns = columns[:, :, margin : margin + tile_cols * side]
    top_half = jnp.pad(columns[:, :side], ((0, 1), (0, 0), (0, 0)))
    bottom_half = jnp.pad(columns[:, side:], ((1, 0), (0, 0), (0, 0)))
    return (top_half + bottom_half).reshape((tile_rows + 1) * side, width)


def per_device(scene, bank, psf_index, psf_weight, response):
    wave_count, tile_rows, tile_cols, side = (
        bank.shape[0],
        bank.shape[1],
        bank.shape[2],
        bank.shape[3],
    )
    entries = psf_index.shape[-1]
    margin = side // 2
    strip = tile_rows * side
    extended = with_halo(bank, (("tile", 1),), 1)
    first_slot = (lax.axis_index("tile") * tile_rows - 1) * tile_cols
    local_slot = psf_index.reshape(tile_rows * tile_cols, entries) - first_slot
    slot_ids = lax.iota(jnp.int32, (tile_rows + 2) * tile_cols)
    fraction = psf_weight.reshape(tile_rows * tile_cols, entries).astype(jnp.float32) / 65536.0
    mixing = jnp.sum(
        jnp.where(local_slot[:, :, None] == slot_ids[None, None, :], fraction[:, :, None], 0.0),
        axis=1,
    )
    tables = dft_tables(side)

    def one_wave(inputs):
        return blur_wave(inputs[0], inputs[1], mixing, tables)

    summed = lax.map(one_wave, (scene, extended))
    from_above = from_behind(summed[:, strip + margin :], "tile", 1)
    from_below = from_behind(summed[:, :margin], "tile", -1)
    blurred = summed[:, margin : margin + strip]
    blurred = blurred.at[:, :margin].add(from_above)
    blurred = blurred.at[:, strip - margin :].add(from_below)
    groups = lax.axis_size("wave")
    width = blurred.shape[-1]
    pieces = blurred.reshape(wave_count, groups, strip // groups, width)
    gathered = lax.all_to_all(pieces, "wave", 1, 1, tiled=True)
    channels = response.shape[0]
    spectral = response.reshape(channels, groups, wave_count)
    colour = jnp.einsum("csi,isrx->crx", spectral, gathered, precision=highest)
    return colour


def solution(mesh):
    in_specs = (
        P("wave", "tile", None),
        P("wave", "tile", None, None, None),
        P("tile", None, None),
        P("tile", None, None),
        P(),
    )
    out_specs = P(None, ("tile", "wave"), None)
    return jax.shard_map(
        per_device, mesh=mesh, in_specs=in_specs, out_specs=out_specs, check_vma=False
    )
```

```python
import math

import jax
import jax.numpy as jnp
from jax import lax
from jax.sharding import PartitionSpec as P

highest = lax.Precision.HIGHEST
high = lax.Precision.HIGH


def with_halo(cells, sides, width):
    for axis, dim in sides:
        count = lax.axis_size(axis)
        ends = count - 1
        head = lax.slice_in_dim(cells, 0, width, axis=dim)
        tail = lax.slice_in_dim(cells, cells.shape[dim] - width, cells.shape[dim], axis=dim)
        cells = jnp.concatenate(
            [
                lax.ppermute(tail, axis, [(i, (i + 1) % count) for i in range(ends)]),
                cells,
                lax.ppermute(head, axis, [((i + 1) % count, i) for i in range(ends)]),
            ],
            axis=dim,
        )
    return cells


def from_behind(shard, axis, by):
    size = lax.axis_size(axis)
    pairs = [(i, i + by) for i in range(size) if 0 <= i + by < size]
    return lax.ppermute(shard, axis, pairs)


def angle_table(rows, cols, length):
    products = lax.iota(jnp.int32, rows)[:, None] * lax.iota(jnp.int32, cols)[None, :] % length
    angles = products.astype(jnp.float32) * (2.0 * math.pi / length)
    return jnp.cos(angles), jnp.sin(angles)


def dft_tables(side):
    length = 2 * side
    half = side
    cos_in, sin_in = angle_table(side, half, length)
    alternating = jnp.where(lax.iota(jnp.int32, side) % 2 == 0, 1.0, -1.0).astype(jnp.float32)
    first = jnp.concatenate([cos_in, (-sin_in).at[:, 0].set(alternating)], axis=1)
    cos_top, sin_top = angle_table(side, length, length)
    rows_fwd = jnp.concatenate([cos_top, sin_top], axis=1)
    cos_full, sin_full = angle_table(length, length, length)
    rows_inv = jnp.concatenate([cos_full, sin_full], axis=1)
    cos_out, sin_out = angle_table(half, length, length)
    every = jnp.where(lax.iota(jnp.int32, length) % 2 == 0, 1.0, -1.0).astype(jnp.float32)
    cos_out = (2.0 * cos_out).at[0].set(1.0)
    sin_out = (-2.0 * sin_out).at[0].set(every)
    last = jnp.concatenate([cos_out, sin_out], axis=0) / float(length * length)
    return first, rows_fwd, rows_inv, last


def forward(blocks, first, rows_fwd):
    half = first.shape[1] // 2
    length = rows_fwd.shape[1] // 2
    packed = jnp.einsum("tab,bj->taj", blocks, first, precision=highest)
    both = jnp.einsum("ak,taj->tkj", rows_fwd, packed, precision=highest)
    by_cos, by_sin = both[:, :length], both[:, length:]
    spec_real = by_cos[..., :half] + by_sin[..., half:]
    spec_imag = by_cos[..., half:] - by_sin[..., :half]
    return spec_real, spec_imag


def reverse(values):
    return jnp.roll(jnp.flip(values, axis=-1), 1, axis=-1)


def split_packed(real, imag):
    real_rev, imag_rev = reverse(real), reverse(imag)
    low = (0.5 * (real + real_rev), 0.5 * (imag - imag_rev))
    top = (0.5 * (imag + imag_rev), -0.5 * (real - real_rev))
    return low, top


def times(a, b):
    return (a[0] * b[0] - a[1] * b[1], a[0] * b[1] + a[1] * b[0])


def product(scene_spec, psf_spec):
    prod_real, prod_imag = times(scene_spec, psf_spec)
    scene_low, scene_top = split_packed(scene_spec[0][..., 0], scene_spec[1][..., 0])
    psf_low, psf_top = split_packed(psf_spec[0][..., 0], psf_spec[1][..., 0])
    low = times(scene_low, psf_low)
    top = times(scene_top, psf_top)
    prod_real = prod_real.at[..., 0].set(low[0] - top[1])
    prod_imag = prod_imag.at[..., 0].set(low[1] + top[0])
    return prod_real, prod_imag


def inverse(prod_real, prod_imag, rows_inv, last):
    half = prod_real.shape[-1]
    length = rows_inv.shape[0]
    stacked = jnp.concatenate([prod_real, prod_imag], axis=-1)
    both = jnp.einsum("km,tkj->tmj", rows_inv, stacked, precision=high)
    by_cos, by_sin = both[:, :length], both[:, length:]
    part_real = by_cos[..., :half] - by_sin[..., half:]
    part_imag = by_sin[..., :half] + by_cos[..., half:]
    packed = jnp.concatenate([part_real, part_imag], axis=-1)
    return jnp.einsum("tmj,jn->tmn", packed, last, precision=high)


def blur_wave(scene_plane, extended_plane, mixing, tables):
    first, rows_fwd, rows_inv, last = tables
    slots, tile_cols, side = (
        extended_plane.shape[0] * extended_plane.shape[1],
        extended_plane.shape[1],
        extended_plane.shape[-1],
    )
    tile_rows = extended_plane.shape[0] - 2
    tiles = tile_rows * tile_cols
    width = scene_plane.shape[1]
    margin = side // 2
    psf_set = jnp.dot(mixing, extended_plane.reshape(slots, side * side), precision=highest)
    psf_set = psf_set.reshape(tiles, side, side)
    tile_set = (
        scene_plane.reshape(tile_rows, side, tile_cols, side)
        .transpose(0, 2, 1, 3)
        .reshape(tiles, side, side)
    )
    spec_real, spec_imag = forward(jnp.concatenate([tile_set, psf_set]), first, rows_fwd)
    prod_real, prod_imag = product(
        (spec_real[:tiles], spec_imag[:tiles]), (spec_real[tiles:], spec_imag[tiles:])
    )
    circular = inverse(prod_real, prod_imag, rows_inv, last)
    circular = circular.reshape(tile_rows, tile_cols, 2 * side, 2 * side)
    left_half = jnp.pad(circular[..., :side], ((0, 0), (0, 1), (0, 0), (0, 0)))
    right_half = jnp.pad(circular[..., side:], ((0, 0), (1, 0), (0, 0), (0, 0)))
    columns = (left_half + right_half).transpose(0, 2, 1, 3)
    columns = columns.reshape(tile_rows, 2 * side, (tile_cols + 1) * side)
    columns = columns[:, :, margin : margin + tile_cols * side]
    top_half = jnp.pad(columns[:, :side], ((0, 1), (0, 0), (0, 0)))
    bottom_half = jnp.pad(columns[:, side:], ((1, 0), (0, 0), (0, 0)))
    return (top_half + bottom_half).reshape((tile_rows + 1) * side, width)


def per_device(scene, bank, psf_index, psf_weight, response):
    wave_count, tile_rows, tile_cols, side = (
        bank.shape[0],
        bank.shape[1],
        bank.shape[2],
        bank.shape[3],
    )
    entries = psf_index.shape[-1]
    margin = side // 2
    strip = tile_rows * side
    extended = with_halo(bank, (("tile", 1),), 1)
    first_slot = (lax.axis_index("tile") * tile_rows - 1) * tile_cols
    local_slot = psf_index.reshape(tile_rows * tile_cols, entries) - first_slot
    slot_ids = lax.iota(jnp.int32, (tile_rows + 2) * tile_cols)
    fraction = psf_weight.reshape(tile_rows * tile_cols, entries).astype(jnp.float32) / 65536.0
    mixing = jnp.sum(
        jnp.where(local_slot[:, :, None] == slot_ids[None, None, :], fraction[:, :, None], 0.0),
        axis=1,
    )
    tables = dft_tables(side)

    def one_wave(inputs):
        return blur_wave(inputs[0], inputs[1], mixing, tables)

    summed = lax.map(one_wave, (scene, extended))
    from_above = from_behind(summed[:, strip + margin :], "tile", 1)
    from_below = from_behind(summed[:, :margin], "tile", -1)
    blurred = summed[:, margin : margin + strip]
    blurred = blurred.at[:, :margin].add(from_above)
    blurred = blurred.at[:, strip - margin :].add(from_below)
    groups = lax.axis_size("wave")
    width = blurred.shape[-1]
    inner = 4 if groups % 4 == 0 else 1
    outer = groups // inner
    pieces = blurred.reshape(wave_count, outer, inner, strip // groups, width)
    across = [[o * inner + i for i in range(inner)] for o in range(outer)]
    along = [[o * inner + i for o in range(outer)] for i in range(inner)]
    pieces = lax.all_to_all(pieces, "wave", 2, 2, tiled=True, axis_index_groups=across)
    pieces = lax.all_to_all(pieces, "wave", 1, 1, tiled=True, axis_index_groups=along)
    gathered = pieces.reshape(wave_count, groups, strip // groups, width)
    channels = response.shape[0]
    spectral = response.reshape(channels, groups, wave_count)
    colour = jnp.einsum("csi,isrx->crx", spectral, gathered, precision=highest)
    return colour


def solution(mesh):
    in_specs = (
        P("wave", "tile", None),
        P("wave", "tile", None, None, None),
        P("tile", None, None),
        P("tile", None, None),
        P(),
    )
    out_specs = P(None, ("tile", "wave"), None)
    return jax.shard_map(
        per_device, mesh=mesh, in_specs=in_specs, out_specs=out_specs, check_vma=False
    )
```

```python
import math

import jax
import jax.numpy as jnp
from jax import lax
from jax.sharding import PartitionSpec as P

highest = lax.Precision.HIGHEST
high = lax.Precision.HIGH


def with_halo(cells, sides, width):
    for axis, dim in sides:
        count = lax.axis_size(axis)
        ends = count - 1
        head = lax.slice_in_dim(cells, 0, width, axis=dim)
        tail = lax.slice_in_dim(cells, cells.shape[dim] - width, cells.shape[dim], axis=dim)
        cells = jnp.concatenate(
            [
                lax.ppermute(tail, axis, [(i, (i + 1) % count) for i in range(ends)]),
                cells,
                lax.ppermute(head, axis, [((i + 1) % count, i) for i in range(ends)]),
            ],
            axis=dim,
        )
    return cells


def from_behind(shard, axis, by):
    size = lax.axis_size(axis)
    pairs = [(i, i + by) for i in range(size) if 0 <= i + by < size]
    return lax.ppermute(shard, axis, pairs)


def angle_table(rows, cols, length):
    products = lax.iota(jnp.int32, rows)[:, None] * lax.iota(jnp.int32, cols)[None, :] % length
    angles = products.astype(jnp.float32) * (2.0 * math.pi / length)
    return jnp.cos(angles), jnp.sin(angles)


def dft_tables(side):
    length = 2 * side
    half = side
    cos_in, sin_in = angle_table(side, half, length)
    alternating = jnp.where(lax.iota(jnp.int32, side) % 2 == 0, 1.0, -1.0).astype(jnp.float32)
    first = jnp.stack([cos_in, (-sin_in).at[:, 0].set(alternating)], axis=1)
    cos_top, sin_top = angle_table(side, length, length)
    rows_fwd = jnp.concatenate(
        [
            jnp.concatenate([cos_top.T, sin_top.T], axis=1),
            jnp.concatenate([-sin_top.T, cos_top.T], axis=1),
        ],
        axis=0,
    )
    cos_full, sin_full = angle_table(length, length, length)
    rows_inv = jnp.concatenate(
        [
            jnp.concatenate([cos_full, -sin_full], axis=1),
            jnp.concatenate([sin_full, cos_full], axis=1),
        ],
        axis=0,
    )
    cos_out, sin_out = angle_table(half, length, length)
    every = jnp.where(lax.iota(jnp.int32, length) % 2 == 0, 1.0, -1.0).astype(jnp.float32)
    cos_out = (2.0 * cos_out).at[0].set(1.0)
    sin_out = (-2.0 * sin_out).at[0].set(every)
    last = jnp.stack([cos_out, sin_out], axis=0) / float(length * length)
    return first, rows_fwd, rows_inv, last


def forward(blocks, first, rows_fwd):
    tiles, side = blocks.shape[0], blocks.shape[1]
    half = first.shape[-1]
    length = rows_fwd.shape[0] // 2
    packed = jnp.einsum("tab,bpl->tpal", blocks, first, precision=highest)
    packed = packed.reshape(tiles, 2 * side, half)
    spec = jnp.einsum("oq,tql->tol", rows_fwd, packed, precision=highest)
    return spec[:, :length], spec[:, length:]


def reverse(values):
    return jnp.roll(jnp.flip(values, axis=-1), 1, axis=-1)


def split_packed(real, imag):
    real_rev, imag_rev = reverse(real), reverse(imag)
    low = (0.5 * (real + real_rev), 0.5 * (imag - imag_rev))
    top = (0.5 * (imag + imag_rev), -0.5 * (real - real_rev))
    return low, top


def times(a, b):
    return (a[0] * b[0] - a[1] * b[1], a[0] * b[1] + a[1] * b[0])


def product(scene_spec, psf_spec):
    prod_real, prod_imag = times(scene_spec, psf_spec)
    scene_low, scene_top = split_packed(scene_spec[0][..., 0], scene_spec[1][..., 0])
    psf_low, psf_top = split_packed(psf_spec[0][..., 0], psf_spec[1][..., 0])
    low = times(scene_low, psf_low)
    top = times(scene_top, psf_top)
    first_column = lax.iota(jnp.int32, prod_real.shape[-1]) == 0
    prod_real = jnp.where(first_column, (low[0] - top[1])[..., None], prod_real)
    prod_imag = jnp.where(first_column, (low[1] + top[0])[..., None], prod_imag)
    return prod_real, prod_imag


def inverse(prod_real, prod_imag, rows_inv, last):
    tiles, length, half = prod_real.shape
    stacked = jnp.concatenate([prod_real, prod_imag], axis=1)
    both = jnp.einsum("oq,tql->tol", rows_inv, stacked, precision=high)
    both = both.reshape(tiles, 2, length, half)
    return jnp.einsum("tpml,pln->tmn", both, last, precision=high)


def blur_wave(scene_plane, extended_plane, mixing, tables):
    first, rows_fwd, rows_inv, last = tables
    slots, tile_cols, side = (
        extended_plane.shape[0] * extended_plane.shape[1],
        extended_plane.shape[1],
        extended_plane.shape[-1],
    )
    tile_rows = extended_plane.shape[0] - 2
    tiles = tile_rows * tile_cols
    width = scene_plane.shape[1]
    margin = side // 2
    psf_set = jnp.dot(mixing, extended_plane.reshape(slots, side * side), precision=highest)
    psf_set = psf_set.reshape(tiles, side, side)
    tile_set = (
        scene_plane.reshape(tile_rows, side, tile_cols, side)
        .transpose(0, 2, 1, 3)
        .reshape(tiles, side, side)
    )
    spec_real, spec_imag = forward(jnp.concatenate([tile_set, psf_set]), first, rows_fwd)
    prod_real, prod_imag = product(
        (spec_real[:tiles], spec_imag[:tiles]), (spec_real[tiles:], spec_imag[tiles:])
    )
    circular = inverse(prod_real, prod_imag, rows_inv, last)
    circular = circular.reshape(tile_rows, tile_cols, 2 * side, 2 * side)
    left_half = jnp.pad(circular[..., :side], ((0, 0), (0, 1), (0, 0), (0, 0)))
    right_half = jnp.pad(circular[..., side:], ((0, 0), (1, 0), (0, 0), (0, 0)))
    columns = (left_half + right_half).transpose(0, 2, 1, 3)
    columns = columns.reshape(tile_rows, 2 * side, (tile_cols + 1) * side)
    columns = columns[:, :, margin : margin + tile_cols * side]
    top_half = jnp.pad(columns[:, :side], ((0, 1), (0, 0), (0, 0)))
    bottom_half = jnp.pad(columns[:, side:], ((1, 0), (0, 0), (0, 0)))
    return (top_half + bottom_half).reshape((tile_rows + 1) * side, width)


def per_device(scene, bank, psf_index, psf_weight, response):
    wave_count, tile_rows, tile_cols, side = (
        bank.shape[0],
        bank.shape[1],
        bank.shape[2],
        bank.shape[3],
    )
    entries = psf_index.shape[-1]
    margin = side // 2
    strip = tile_rows * side
    extended = with_halo(bank, (("tile", 1),), 1)
    first_slot = (lax.axis_index("tile") * tile_rows - 1) * tile_cols
    local_slot = psf_index.reshape(tile_rows * tile_cols, entries) - first_slot
    slot_ids = lax.iota(jnp.int32, (tile_rows + 2) * tile_cols)
    fraction = psf_weight.reshape(tile_rows * tile_cols, entries).astype(jnp.float32) / 65536.0
    mixing = jnp.sum(
        jnp.where(local_slot[:, :, None] == slot_ids[None, None, :], fraction[:, :, None], 0.0),
        axis=1,
    )
    tables = dft_tables(side)

    def one_wave(inputs):
        return blur_wave(inputs[0], inputs[1], mixing, tables)

    summed = lax.map(one_wave, (scene, extended))
    from_above = from_behind(summed[:, strip + margin :], "tile", 1)
    from_below = from_behind(summed[:, :margin], "tile", -1)
    blurred = summed[:, margin : margin + strip]
    blurred = blurred.at[:, :margin].add(from_above)
    blurred = blurred.at[:, strip - margin :].add(from_below)
    groups = lax.axis_size("wave")
    width = blurred.shape[-1]
    pieces = blurred.reshape(wave_count, groups, strip // groups, width)
    gathered = lax.all_to_all(pieces, "wave", 1, 1, tiled=True)
    channels = response.shape[0]
    spectral = response.reshape(channels, groups, wave_count)
    colour = jnp.einsum("csi,isrx->crx", spectral, gathered, precision=highest)
    return colour


def solution(mesh):
    in_specs = (
        P("wave", "tile", None),
        P("wave", "tile", None, None, None),
        P("tile", None, None),
        P("tile", None, None),
        P(),
    )
    out_specs = P(None, ("tile", "wave"), None)
    return jax.shard_map(
        per_device, mesh=mesh, in_specs=in_specs, out_specs=out_specs, check_vma=False
    )
```

```python
import math

import jax
import jax.numpy as jnp
from jax import lax
from jax.sharding import PartitionSpec as P

highest = lax.Precision.HIGHEST
high = lax.Precision.HIGH


def with_halo(cells, sides, width):
    for axis, dim in sides:
        count = lax.axis_size(axis)
        ends = count - 1
        head = lax.slice_in_dim(cells, 0, width, axis=dim)
        tail = lax.slice_in_dim(cells, cells.shape[dim] - width, cells.shape[dim], axis=dim)
        cells = jnp.concatenate(
            [
                lax.ppermute(tail, axis, [(i, (i + 1) % count) for i in range(ends)]),
                cells,
                lax.ppermute(head, axis, [((i + 1) % count, i) for i in range(ends)]),
            ],
            axis=dim,
        )
    return cells


def from_behind(shard, axis, by):
    size = lax.axis_size(axis)
    pairs = [(i, i + by) for i in range(size) if 0 <= i + by < size]
    return lax.ppermute(shard, axis, pairs)


def angle_table(rows, cols, length):
    products = lax.iota(jnp.int32, rows)[:, None] * lax.iota(jnp.int32, cols)[None, :] % length
    angles = products.astype(jnp.float32) * (2.0 * math.pi / length)
    return jnp.cos(angles), jnp.sin(angles)


def dft_tables(side):
    length = 2 * side
    half = side
    cos_in, sin_in = angle_table(side, half, length)
    alternating = jnp.where(lax.iota(jnp.int32, side) % 2 == 0, 1.0, -1.0).astype(jnp.float32)
    first = jnp.stack([cos_in, (-sin_in).at[:, 0].set(alternating)], axis=1)
    cos_top, sin_top = angle_table(side, length, length)
    rows_fwd = jnp.concatenate(
        [
            jnp.concatenate([cos_top.T, sin_top.T], axis=1),
            jnp.concatenate([-sin_top.T, cos_top.T], axis=1),
        ],
        axis=0,
    )
    cos_full, sin_full = angle_table(length, length, length)
    rows_inv = jnp.concatenate(
        [
            jnp.concatenate([cos_full, -sin_full], axis=1),
            jnp.concatenate([sin_full, cos_full], axis=1),
        ],
        axis=0,
    )
    cos_out, sin_out = angle_table(half, length, length)
    every = jnp.where(lax.iota(jnp.int32, length) % 2 == 0, 1.0, -1.0).astype(jnp.float32)
    cos_out = (2.0 * cos_out).at[0].set(1.0)
    sin_out = (-2.0 * sin_out).at[0].set(every)
    last = jnp.stack([cos_out, sin_out], axis=0) / float(length * length)
    return first, rows_fwd, rows_inv, last


def forward(blocks, first, rows_fwd):
    tiles = blocks.shape[0]
    half = first.shape[-1]
    length = rows_fwd.shape[0] // 2
    first = first.transpose(0, 2, 1).reshape(first.shape[0], 2 * half)
    packed = jnp.einsum("tab,bj->tja", blocks, first, precision=highest)
    packed = packed.reshape(tiles, half, rows_fwd.shape[1])
    spec = jnp.einsum("tlq,oq->tlo", packed, rows_fwd, precision=highest)
    return spec[..., :length], spec[..., length:]


def reverse(values):
    return jnp.roll(jnp.flip(values, axis=-1), 1, axis=-1)


def split_packed(real, imag):
    real_rev, imag_rev = reverse(real), reverse(imag)
    low = (0.5 * (real + real_rev), 0.5 * (imag - imag_rev))
    top = (0.5 * (imag + imag_rev), -0.5 * (real - real_rev))
    return low, top


def times(a, b):
    return (a[0] * b[0] - a[1] * b[1], a[0] * b[1] + a[1] * b[0])


def product(scene_spec, psf_spec):
    prod_real, prod_imag = times(scene_spec, psf_spec)
    scene_low, scene_top = split_packed(scene_spec[0][:, 0], scene_spec[1][:, 0])
    psf_low, psf_top = split_packed(psf_spec[0][:, 0], psf_spec[1][:, 0])
    low = times(scene_low, psf_low)
    top = times(scene_top, psf_top)
    first_column = (lax.iota(jnp.int32, prod_real.shape[1]) == 0)[:, None]
    prod_real = jnp.where(first_column, (low[0] - top[1])[:, None, :], prod_real)
    prod_imag = jnp.where(first_column, (low[1] + top[0])[:, None, :], prod_imag)
    return prod_real, prod_imag


def inverse(prod_real, prod_imag, rows_inv, last):
    tiles, half, length = prod_real.shape
    stacked = jnp.concatenate([prod_real, prod_imag], axis=-1)
    rows_inv = rows_inv.reshape(2, length, 2 * length).transpose(1, 0, 2).reshape(2 * length, 2 * length)
    both = jnp.einsum("tlq,oq->tol", stacked, rows_inv, precision=high)
    both = both.reshape(tiles, length, 2 * half)
    return jnp.einsum("tmj,jn->tmn", both, last.reshape(2 * half, length), precision=high)


def blur_wave(scene_plane, extended_plane, mixing, tables):
    first, rows_fwd, rows_inv, last = tables
    slots, tile_cols, side = (
        extended_plane.shape[0] * extended_plane.shape[1],
        extended_plane.shape[1],
        extended_plane.shape[-1],
    )
    tile_rows = extended_plane.shape[0] - 2
    tiles = tile_rows * tile_cols
    width = scene_plane.shape[1]
    margin = side // 2
    psf_set = jnp.dot(mixing, extended_plane.reshape(slots, side * side), precision=highest)
    psf_set = psf_set.reshape(tiles, side, side)
    tile_set = (
        scene_plane.reshape(tile_rows, side, tile_cols, side)
        .transpose(0, 2, 1, 3)
        .reshape(tiles, side, side)
    )
    spec_real, spec_imag = forward(jnp.concatenate([tile_set, psf_set]), first, rows_fwd)
    prod_real, prod_imag = product(
        (spec_real[:tiles], spec_imag[:tiles]), (spec_real[tiles:], spec_imag[tiles:])
    )
    circular = inverse(prod_real, prod_imag, rows_inv, last)
    circular = circular.reshape(tile_rows, tile_cols, 2 * side, 2 * side)
    left_half = jnp.pad(circular[..., :side], ((0, 0), (0, 1), (0, 0), (0, 0)))
    right_half = jnp.pad(circular[..., side:], ((0, 0), (1, 0), (0, 0), (0, 0)))
    columns = (left_half + right_half).transpose(0, 2, 1, 3)
    columns = columns.reshape(tile_rows, 2 * side, (tile_cols + 1) * side)
    columns = columns[:, :, margin : margin + tile_cols * side]
    top_half = jnp.pad(columns[:, :side], ((0, 1), (0, 0), (0, 0)))
    bottom_half = jnp.pad(columns[:, side:], ((1, 0), (0, 0), (0, 0)))
    return (top_half + bottom_half).reshape((tile_rows + 1) * side, width)


def per_device(scene, bank, psf_index, psf_weight, response):
    wave_count, tile_rows, tile_cols, side = (
        bank.shape[0],
        bank.shape[1],
        bank.shape[2],
        bank.shape[3],
    )
    entries = psf_index.shape[-1]
    margin = side // 2
    strip = tile_rows * side
    extended = with_halo(bank, (("tile", 1),), 1)
    first_slot = (lax.axis_index("tile") * tile_rows - 1) * tile_cols
    local_slot = psf_index.reshape(tile_rows * tile_cols, entries) - first_slot
    slot_ids = lax.iota(jnp.int32, (tile_rows + 2) * tile_cols)
    fraction = psf_weight.reshape(tile_rows * tile_cols, entries).astype(jnp.float32) / 65536.0
    mixing = jnp.sum(
        jnp.where(local_slot[:, :, None] == slot_ids[None, None, :], fraction[:, :, None], 0.0),
        axis=1,
    )
    tables = dft_tables(side)

    def one_wave(inputs):
        return blur_wave(inputs[0], inputs[1], mixing, tables)

    summed = lax.map(one_wave, (scene, extended))
    from_above = from_behind(summed[:, strip + margin :], "tile", 1)
    from_below = from_behind(summed[:, :margin], "tile", -1)
    blurred = summed[:, margin : margin + strip]
    blurred = blurred.at[:, :margin].add(from_above)
    blurred = blurred.at[:, strip - margin :].add(from_below)
    groups = lax.axis_size("wave")
    width = blurred.shape[-1]
    pieces = blurred.reshape(wave_count, groups, strip // groups, width)
    gathered = lax.all_to_all(pieces, "wave", 1, 1, tiled=True)
    channels = response.shape[0]
    spectral = response.reshape(channels, groups, wave_count)
    colour = jnp.einsum("csi,isrx->crx", spectral, gathered, precision=highest)
    return colour


def solution(mesh):
    in_specs = (
        P("wave", "tile", None),
        P("wave", "tile", None, None, None),
        P("tile", None, None),
        P("tile", None, None),
        P(),
    )
    out_specs = P(None, ("tile", "wave"), None)
    return jax.shard_map(
        per_device, mesh=mesh, in_specs=in_specs, out_specs=out_specs, check_vma=False
    )
```

```python
import math

import jax
import jax.numpy as jnp
from jax import lax
from jax.sharding import PartitionSpec as P

highest = lax.Precision.HIGHEST
high = lax.Precision.HIGH


def with_halo(cells, sides, width):
    for axis, dim in sides:
        count = lax.axis_size(axis)
        ends = count - 1
        head = lax.slice_in_dim(cells, 0, width, axis=dim)
        tail = lax.slice_in_dim(cells, cells.shape[dim] - width, cells.shape[dim], axis=dim)
        cells = jnp.concatenate(
            [
                lax.ppermute(tail, axis, [(i, (i + 1) % count) for i in range(ends)]),
                cells,
                lax.ppermute(head, axis, [((i + 1) % count, i) for i in range(ends)]),
            ],
            axis=dim,
        )
    return cells


def from_behind(shard, axis, by):
    size = lax.axis_size(axis)
    pairs = [(i, i + by) for i in range(size) if 0 <= i + by < size]
    return lax.ppermute(shard, axis, pairs)


def angle_table(rows, cols, length):
    products = lax.iota(jnp.int32, rows)[:, None] * lax.iota(jnp.int32, cols)[None, :] % length
    angles = products.astype(jnp.float32) * (2.0 * math.pi / length)
    return jnp.cos(angles), jnp.sin(angles)


def dft_tables(side):
    length = 2 * side
    cos_full, sin_full = angle_table(length, length, length)
    first_row = (lax.iota(jnp.int32, side) == 0)
    signs = jnp.where(lax.iota(jnp.int32, length) % 2 == 0, 1.0, -1.0).astype(jnp.float32)
    cos_in, sin_in = cos_full[:side, :side], sin_full[:side, :side]
    first = jnp.stack([cos_in, jnp.where(first_row[None, :], signs[:side, None], -sin_in)], axis=1)
    cos_k, sin_k = cos_full[:, :side], sin_full[:, :side]
    rows_fwd = jnp.stack(
        [jnp.stack([cos_k, sin_k], axis=1), jnp.stack([-sin_k, cos_k], axis=1)], axis=0
    ).reshape(2 * length, 2, side)
    rows_inv = jnp.concatenate(
        [
            jnp.concatenate([cos_full, -sin_full], axis=1),
            jnp.concatenate([sin_full, cos_full], axis=1),
        ],
        axis=0,
    )
    cos_out = jnp.where(first_row[:, None], 1.0, 2.0 * cos_full[:side])
    sin_out = jnp.where(first_row[:, None], signs[None, :], -2.0 * sin_full[:side])
    last = jnp.stack([cos_out, sin_out], axis=0) / float(length * length)
    return first, rows_fwd, rows_inv, last


def forward(blocks, first, rows_fwd):
    side = blocks.shape[1]
    length = rows_fwd.shape[0] // 2
    packed = jnp.einsum("tab,bpl->tpla", blocks, first, precision=highest)
    rows_fwd = rows_fwd.reshape(2 * length, 2, side)
    spec = jnp.einsum("tpla,opa->tlo", packed, rows_fwd, precision=highest)
    return spec[..., :length], spec[..., length:]


def reverse(values):
    return jnp.roll(jnp.flip(values, axis=-1), 1, axis=-1)


def split_packed(real, imag):
    real_rev, imag_rev = reverse(real), reverse(imag)
    low = (0.5 * (real + real_rev), 0.5 * (imag - imag_rev))
    top = (0.5 * (imag + imag_rev), -0.5 * (real - real_rev))
    return low, top


def times(a, b):
    return (a[0] * b[0] - a[1] * b[1], a[0] * b[1] + a[1] * b[0])


def product(scene_spec, psf_spec):
    prod_real, prod_imag = times(scene_spec, psf_spec)
    scene_low, scene_top = split_packed(scene_spec[0][:, 0], scene_spec[1][:, 0])
    psf_low, psf_top = split_packed(psf_spec[0][:, 0], psf_spec[1][:, 0])
    low = times(scene_low, psf_low)
    top = times(scene_top, psf_top)
    first_column = (lax.iota(jnp.int32, prod_real.shape[1]) == 0)[:, None]
    prod_real = jnp.where(first_column, (low[0] - top[1])[:, None, :], prod_real)
    prod_imag = jnp.where(first_column, (low[1] + top[0])[:, None, :], prod_imag)
    return prod_real, prod_imag


def inverse(prod_real, prod_imag, rows_inv, last):
    tiles, half, length = prod_real.shape
    stacked = jnp.concatenate([prod_real, prod_imag], axis=-1)
    both = jnp.einsum("tlq,oq->tol", stacked, rows_inv, precision=high)
    both = both.reshape(tiles, 2, length, half)
    return jnp.einsum("tpml,pln->tmn", both, last, precision=high)


def blur_wave(scene_plane, extended_plane, mixing, tables):
    first, rows_fwd, rows_inv, last = tables
    slots, tile_cols, side = (
        extended_plane.shape[0] * extended_plane.shape[1],
        extended_plane.shape[1],
        extended_plane.shape[-1],
    )
    tile_rows = extended_plane.shape[0] - 2
    tiles = tile_rows * tile_cols
    width = scene_plane.shape[1]
    margin = side // 2
    psf_set = jnp.dot(mixing, extended_plane.reshape(slots, side * side), precision=highest)
    psf_set = psf_set.reshape(tiles, side, side)
    tile_set = (
        scene_plane.reshape(tile_rows, side, tile_cols, side)
        .transpose(0, 2, 1, 3)
        .reshape(tiles, side, side)
    )
    spec_real, spec_imag = forward(jnp.concatenate([tile_set, psf_set]), first, rows_fwd)
    prod_real, prod_imag = product(
        (spec_real[:tiles], spec_imag[:tiles]), (spec_real[tiles:], spec_imag[tiles:])
    )
    circular = inverse(prod_real, prod_imag, rows_inv, last)
    circular = circular.reshape(tile_rows, tile_cols, 2 * side, 2 * side)
    left_half = jnp.pad(circular[..., :side], ((0, 0), (0, 1), (0, 0), (0, 0)))
    right_half = jnp.pad(circular[..., side:], ((0, 0), (1, 0), (0, 0), (0, 0)))
    columns = (left_half + right_half).transpose(0, 2, 1, 3)
    columns = columns.reshape(tile_rows, 2 * side, (tile_cols + 1) * side)
    columns = columns[:, :, margin : margin + tile_cols * side]
    top_half = jnp.pad(columns[:, :side], ((0, 1), (0, 0), (0, 0)))
    bottom_half = jnp.pad(columns[:, side:], ((1, 0), (0, 0), (0, 0)))
    return (top_half + bottom_half).reshape((tile_rows + 1) * side, width)


def per_device(scene, bank, psf_index, psf_weight, response):
    wave_count, tile_rows, tile_cols, side = (
        bank.shape[0],
        bank.shape[1],
        bank.shape[2],
        bank.shape[3],
    )
    entries = psf_index.shape[-1]
    margin = side // 2
    strip = tile_rows * side
    extended = with_halo(bank, (("tile", 1),), 1)
    first_slot = (lax.axis_index("tile") * tile_rows - 1) * tile_cols
    local_slot = psf_index.reshape(tile_rows * tile_cols, entries) - first_slot
    slot_ids = lax.iota(jnp.int32, (tile_rows + 2) * tile_cols)
    fraction = psf_weight.reshape(tile_rows * tile_cols, entries).astype(jnp.float32) / 65536.0
    mixing = jnp.sum(
        jnp.where(local_slot[:, :, None] == slot_ids[None, None, :], fraction[:, :, None], 0.0),
        axis=1,
    )
    tables = dft_tables(side)

    def one_wave(inputs):
        return blur_wave(inputs[0], inputs[1], mixing, tables)

    summed = lax.map(one_wave, (scene, extended))
    from_above = from_behind(summed[:, strip + margin :], "tile", 1)
    from_below = from_behind(summed[:, :margin], "tile", -1)
    blurred = summed[:, margin : margin + strip]
    blurred = blurred.at[:, :margin].add(from_above)
    blurred = blurred.at[:, strip - margin :].add(from_below)
    groups = lax.axis_size("wave")
    width = blurred.shape[-1]
    pieces = blurred.reshape(wave_count, groups, strip // groups, width)
    gathered = lax.all_to_all(pieces, "wave", 1, 1, tiled=True)
    channels = response.shape[0]
    spectral = response.reshape(channels, groups, wave_count)
    colour = jnp.einsum("csi,isrx->crx", spectral, gathered, precision=highest)
    return colour


def solution(mesh):
    in_specs = (
        P("wave", "tile", None),
        P("wave", "tile", None, None, None),
        P("tile", None, None),
        P("tile", None, None),
        P(),
    )
    out_specs = P(None, ("tile", "wave"), None)
    return jax.shard_map(
        per_device, mesh=mesh, in_specs=in_specs, out_specs=out_specs, check_vma=False
    )
```

```python
import math

import jax
import jax.numpy as jnp
from jax import lax
from jax.sharding import PartitionSpec as P

highest = lax.Precision.HIGHEST
high = lax.Precision.HIGH


def with_halo(cells, sides, width):
    for axis, dim in sides:
        count = lax.axis_size(axis)
        ends = count - 1
        head = lax.slice_in_dim(cells, 0, width, axis=dim)
        tail = lax.slice_in_dim(cells, cells.shape[dim] - width, cells.shape[dim], axis=dim)
        cells = jnp.concatenate(
            [
                lax.ppermute(tail, axis, [(i, (i + 1) % count) for i in range(ends)]),
                cells,
                lax.ppermute(head, axis, [((i + 1) % count, i) for i in range(ends)]),
            ],
            axis=dim,
        )
    return cells


def from_behind(shard, axis, by):
    size = lax.axis_size(axis)
    pairs = [(i, i + by) for i in range(size) if 0 <= i + by < size]
    return lax.ppermute(shard, axis, pairs)


def angle_table(rows, cols, length):
    products = lax.iota(jnp.int32, rows)[:, None] * lax.iota(jnp.int32, cols)[None, :] % length
    angles = products.astype(jnp.float32) * (2.0 * math.pi / length)
    return jnp.cos(angles), jnp.sin(angles)


def dft_tables(side):
    length = 2 * side
    cos_full, sin_full = angle_table(length, length, length)
    first_row = (lax.iota(jnp.int32, side) == 0)
    signs = jnp.where(lax.iota(jnp.int32, length) % 2 == 0, 1.0, -1.0).astype(jnp.float32)
    cos_in, sin_in = cos_full[:side, :side], sin_full[:side, :side]
    first = jnp.stack([cos_in, jnp.where(first_row[None, :], signs[:side, None], -sin_in)], axis=1)
    cos_k, sin_k = cos_full[:, :side], sin_full[:, :side]
    rows_fwd = jnp.stack(
        [jnp.stack([cos_k, sin_k], axis=1), jnp.stack([-sin_k, cos_k], axis=1)], axis=0
    ).reshape(2 * length, 2, side)
    rows_inv = jnp.concatenate(
        [
            jnp.concatenate([cos_full, -sin_full], axis=1),
            jnp.concatenate([sin_full, cos_full], axis=1),
        ],
        axis=0,
    )
    cos_out = jnp.where(first_row[:, None], 1.0, 2.0 * cos_full[:side])
    sin_out = jnp.where(first_row[:, None], signs[None, :], -2.0 * sin_full[:side])
    last = jnp.stack([cos_out, sin_out], axis=0) / float(length * length)
    return first, rows_fwd, rows_inv, last


def forward(blocks, first, rows_fwd):
    side = blocks.shape[1]
    length = rows_fwd.shape[0] // 2
    packed = jnp.einsum("tab,bpl->tpla", blocks, first, precision=highest)
    rows_fwd = rows_fwd.reshape(2 * length, 2, side)
    spec = jnp.einsum("tpla,opa->tlo", packed, rows_fwd, precision=highest)
    return spec[..., :length], spec[..., length:]


def reverse(values):
    return jnp.roll(jnp.flip(values, axis=-1), 1, axis=-1)


def split_packed(real, imag):
    real_rev, imag_rev = reverse(real), reverse(imag)
    low = (0.5 * (real + real_rev), 0.5 * (imag - imag_rev))
    top = (0.5 * (imag + imag_rev), -0.5 * (real - real_rev))
    return low, top


def times(a, b):
    return (a[0] * b[0] - a[1] * b[1], a[0] * b[1] + a[1] * b[0])


def product(scene_spec, psf_spec):
    prod_real, prod_imag = times(scene_spec, psf_spec)
    scene_low, scene_top = split_packed(scene_spec[0][:, 0], scene_spec[1][:, 0])
    psf_low, psf_top = split_packed(psf_spec[0][:, 0], psf_spec[1][:, 0])
    low = times(scene_low, psf_low)
    top = times(scene_top, psf_top)
    first_column = (lax.iota(jnp.int32, prod_real.shape[1]) == 0)[:, None]
    prod_real = jnp.where(first_column, (low[0] - top[1])[:, None, :], prod_real)
    prod_imag = jnp.where(first_column, (low[1] + top[0])[:, None, :], prod_imag)
    return prod_real, prod_imag


def inverse(prod_real, prod_imag, rows_inv, last):
    tiles, half, length = prod_real.shape
    stacked = jnp.concatenate([prod_real, prod_imag], axis=-1)
    both = jnp.einsum("tlq,oq->tol", stacked, rows_inv, precision=high)
    both = both.reshape(tiles, 2, length, half)
    return jnp.einsum("tpml,pln->tmn", both, last, precision=high)


def column_sum(circular, side, width):
    tile_cols = circular.shape[0]
    margin = side // 2
    left_half = jnp.pad(circular[..., :side], ((0, 1), (0, 0), (0, 0)))
    right_half = jnp.pad(circular[..., side:], ((1, 0), (0, 0), (0, 0)))
    columns = (left_half + right_half).transpose(1, 0, 2)
    columns = columns.reshape(circular.shape[1], (tile_cols + 1) * side)
    return columns[:, margin : margin + width]


def blur_wave(scene_plane, extended_plane, mixing, tables):
    first, rows_fwd, rows_inv, last = tables
    slots, tile_cols, side = (
        extended_plane.shape[0] * extended_plane.shape[1],
        extended_plane.shape[1],
        extended_plane.shape[-1],
    )
    tile_rows = extended_plane.shape[0] - 2
    tiles = tile_rows * tile_cols
    width = scene_plane.shape[1]
    margin = side // 2
    length = 2 * side
    tile_set = (
        scene_plane.reshape(tile_rows, side, tile_cols, side)
        .transpose(0, 2, 1, 3)
        .reshape(tiles, side, side)
    )
    scene_spec = forward(tile_set, first, rows_fwd)
    psf_set = jnp.dot(mixing, extended_plane.reshape(slots, side * side), precision=highest)
    psf_spec = forward(psf_set.reshape(tiles, side, side), first, rows_fwd)
    prod_real, prod_imag = product(scene_spec, psf_spec)
    stacked = jnp.concatenate([prod_real, prod_imag], axis=-1)
    both = jnp.einsum("tlq,oq->tol", stacked, rows_inv, precision=high)
    both = both.reshape(tile_rows, tile_cols, 2, length, side)

    def rows_of(row, lo, hi):
        part = jnp.einsum("cpml,pln->cmn", both[row, :, :, lo:hi], last, precision=high)
        return column_sum(part, side, width)

    up = rows_of(0, 0, margin)
    down = rows_of(tile_rows - 1, length - margin, length)
    strip = tile_rows * side
    blurred = jnp.zeros((strip, width), jnp.float32)
    for row in range(tile_rows):
        lo = margin if row == 0 else 0
        hi = length - margin if row == tile_rows - 1 else length
        at = row * side + lo - margin
        blurred = blurred.at[at : at + hi - lo].add(rows_of(row, lo, hi))
    return blurred, up, down


def per_device(scene, bank, psf_index, psf_weight, response):
    wave_count, tile_rows, tile_cols, side = (
        bank.shape[0],
        bank.shape[1],
        bank.shape[2],
        bank.shape[3],
    )
    entries = psf_index.shape[-1]
    margin = side // 2
    strip = tile_rows * side
    extended = with_halo(bank, (("tile", 1),), 1)
    first_slot = (lax.axis_index("tile") * tile_rows - 1) * tile_cols
    local_slot = psf_index.reshape(tile_rows * tile_cols, entries) - first_slot
    slot_ids = lax.iota(jnp.int32, (tile_rows + 2) * tile_cols)
    fraction = psf_weight.reshape(tile_rows * tile_cols, entries).astype(jnp.float32) / 65536.0
    mixing = jnp.sum(
        jnp.where(local_slot[:, :, None] == slot_ids[None, None, :], fraction[:, :, None], 0.0),
        axis=1,
    )
    tables = dft_tables(side)

    def one_wave(inputs):
        return blur_wave(inputs[0], inputs[1], mixing, tables)

    blurred, up, down = lax.map(one_wave, (scene, extended))
    from_above = from_behind(down, "tile", 1)
    from_below = from_behind(up, "tile", -1)
    blurred = blurred.at[:, :margin].add(from_above)
    blurred = blurred.at[:, strip - margin :].add(from_below)
    groups = lax.axis_size("wave")
    width = blurred.shape[-1]
    pieces = blurred.reshape(wave_count, groups, strip // groups, width)
    gathered = lax.all_to_all(pieces, "wave", 1, 1, tiled=True)
    channels = response.shape[0]
    spectral = response.reshape(channels, groups, wave_count)
    colour = jnp.einsum("csi,isrx->crx", spectral, gathered, precision=highest)
    return colour


def solution(mesh):
    in_specs = (
        P("wave", "tile", None),
        P("wave", "tile", None, None, None),
        P("tile", None, None),
        P("tile", None, None),
        P(),
    )
    out_specs = P(None, ("tile", "wave"), None)
    return jax.shard_map(
        per_device, mesh=mesh, in_specs=in_specs, out_specs=out_specs, check_vma=False
    )
```

```python
import math

import jax
import jax.numpy as jnp
from jax import lax
from jax.sharding import PartitionSpec as P

highest = lax.Precision.HIGHEST
high = lax.Precision.HIGH


def with_halo(cells, sides, width):
    for axis, dim in sides:
        count = lax.axis_size(axis)
        ends = count - 1
        head = lax.slice_in_dim(cells, 0, width, axis=dim)
        tail = lax.slice_in_dim(cells, cells.shape[dim] - width, cells.shape[dim], axis=dim)
        cells = jnp.concatenate(
            [
                lax.ppermute(tail, axis, [(i, (i + 1) % count) for i in range(ends)]),
                cells,
                lax.ppermute(head, axis, [((i + 1) % count, i) for i in range(ends)]),
            ],
            axis=dim,
        )
    return cells


def from_behind(shard, axis, by):
    size = lax.axis_size(axis)
    pairs = [(i, i + by) for i in range(size) if 0 <= i + by < size]
    return lax.ppermute(shard, axis, pairs)


def angle_table(rows, cols, length):
    products = lax.iota(jnp.int32, rows)[:, None] * lax.iota(jnp.int32, cols)[None, :] % length
    angles = products.astype(jnp.float32) * (2.0 * math.pi / length)
    return jnp.cos(angles), jnp.sin(angles)


def dft_tables(side):
    length = 2 * side
    cos_full, sin_full = angle_table(length, length, length)
    first_row = (lax.iota(jnp.int32, side) == 0)
    signs = jnp.where(lax.iota(jnp.int32, length) % 2 == 0, 1.0, -1.0).astype(jnp.float32)
    cos_in, sin_in = cos_full[:side, :side], sin_full[:side, :side]
    first = jnp.stack([cos_in, jnp.where(first_row[None, :], signs[:side, None], -sin_in)], axis=1)
    cos_k, sin_k = cos_full[:, :side], sin_full[:, :side]
    rows_fwd = jnp.stack(
        [jnp.stack([cos_k, sin_k], axis=1), jnp.stack([-sin_k, cos_k], axis=1)], axis=0
    ).reshape(2 * length, 2, side)
    rows_inv = jnp.concatenate(
        [
            jnp.concatenate([cos_full, -sin_full], axis=1),
            jnp.concatenate([sin_full, cos_full], axis=1),
        ],
        axis=0,
    )
    cos_out = jnp.where(first_row[:, None], 1.0, 2.0 * cos_full[:side])
    sin_out = jnp.where(first_row[:, None], signs[None, :], -2.0 * sin_full[:side])
    last = jnp.stack([cos_out, sin_out], axis=0) / float(length * length)
    return first, rows_fwd, rows_inv, last


def forward(blocks, first, rows_fwd):
    side = blocks.shape[1]
    length = rows_fwd.shape[0] // 2
    packed = jnp.einsum("tab,bpl->tpla", blocks, first, precision=highest)
    rows_fwd = rows_fwd.reshape(2 * length, 2, side)
    spec = jnp.einsum("tpla,opa->tlo", packed, rows_fwd, precision=highest)
    return spec[..., :length], spec[..., length:]


def reverse(values):
    return jnp.roll(jnp.flip(values, axis=-1), 1, axis=-1)


def split_packed(real, imag):
    real_rev, imag_rev = reverse(real), reverse(imag)
    low = (0.5 * (real + real_rev), 0.5 * (imag - imag_rev))
    top = (0.5 * (imag + imag_rev), -0.5 * (real - real_rev))
    return low, top


def times(a, b):
    return (a[0] * b[0] - a[1] * b[1], a[0] * b[1] + a[1] * b[0])


def product(scene_spec, psf_spec):
    prod_real, prod_imag = times(scene_spec, psf_spec)
    scene_low, scene_top = split_packed(scene_spec[0][:, 0], scene_spec[1][:, 0])
    psf_low, psf_top = split_packed(psf_spec[0][:, 0], psf_spec[1][:, 0])
    low = times(scene_low, psf_low)
    top = times(scene_top, psf_top)
    first_column = (lax.iota(jnp.int32, prod_real.shape[1]) == 0)[:, None]
    prod_real = jnp.where(first_column, (low[0] - top[1])[:, None, :], prod_real)
    prod_imag = jnp.where(first_column, (low[1] + top[0])[:, None, :], prod_imag)
    return prod_real, prod_imag


def inverse(prod_real, prod_imag, rows_inv, last):
    tiles, half, length = prod_real.shape
    stacked = jnp.concatenate([prod_real, prod_imag], axis=-1)
    both = jnp.einsum("tlq,oq->tol", stacked, rows_inv, precision=high)
    both = both.reshape(tiles, 2, length, half)
    return jnp.einsum("tpml,pln->tmn", both, last, precision=high)


def column_sum(circular, side, width):
    tile_cols = circular.shape[0]
    margin = side // 2
    left_half = jnp.pad(circular[..., :side], ((0, 1), (0, 0), (0, 0)))
    right_half = jnp.pad(circular[..., side:], ((1, 0), (0, 0), (0, 0)))
    columns = (left_half + right_half).transpose(1, 0, 2)
    columns = columns.reshape(circular.shape[1], (tile_cols + 1) * side)
    return columns[:, margin : margin + width]


def blur_wave(scene_plane, extended_plane, mixing, tables):
    first, rows_fwd, rows_inv, last = tables
    slots, tile_cols, side = (
        extended_plane.shape[0] * extended_plane.shape[1],
        extended_plane.shape[1],
        extended_plane.shape[-1],
    )
    tile_rows = extended_plane.shape[0] - 2
    tiles = tile_rows * tile_cols
    width = scene_plane.shape[1]
    margin = side // 2
    length = 2 * side
    tile_set = (
        scene_plane.reshape(tile_rows, side, tile_cols, side)
        .transpose(0, 2, 1, 3)
        .reshape(tiles, side, side)
    )
    scene_spec = forward(tile_set, first, rows_fwd)
    psf_set = jnp.dot(mixing, extended_plane.reshape(slots, side * side), precision=highest)
    psf_spec = forward(psf_set.reshape(tiles, side, side), first, rows_fwd)
    prod_real, prod_imag = product(scene_spec, psf_spec)
    stacked = jnp.concatenate([prod_real, prod_imag], axis=-1)
    both = jnp.einsum("tlq,oq->tol", stacked, rows_inv, precision=high)
    both = both.reshape(tile_rows, tile_cols, 2, length, side)

    def rows_of(row, lo, hi):
        part = jnp.einsum("cpml,pln->cmn", both[row, :, :, lo:hi], last, precision=high)
        return column_sum(part, side, width)

    up = rows_of(0, 0, margin)
    down = rows_of(tile_rows - 1, length - margin, length)
    strip = tile_rows * side
    bands = []
    for row in range(tile_rows):
        lo = margin if row == 0 else 0
        hi = length - margin if row == tile_rows - 1 else length
        at = row * side + lo - margin
        bands.append(jnp.pad(rows_of(row, lo, hi), ((at, strip - at - (hi - lo)), (0, 0))))
    blurred = sum(bands[1:], bands[0])
    return blurred, up, down


def per_device(scene, bank, psf_index, psf_weight, response):
    wave_count, tile_rows, tile_cols, side = (
        bank.shape[0],
        bank.shape[1],
        bank.shape[2],
        bank.shape[3],
    )
    entries = psf_index.shape[-1]
    margin = side // 2
    strip = tile_rows * side
    extended = with_halo(bank, (("tile", 1),), 1)
    first_slot = (lax.axis_index("tile") * tile_rows - 1) * tile_cols
    local_slot = psf_index.reshape(tile_rows * tile_cols, entries) - first_slot
    slot_ids = lax.iota(jnp.int32, (tile_rows + 2) * tile_cols)
    fraction = psf_weight.reshape(tile_rows * tile_cols, entries).astype(jnp.float32) / 65536.0
    mixing = jnp.sum(
        jnp.where(local_slot[:, :, None] == slot_ids[None, None, :], fraction[:, :, None], 0.0),
        axis=1,
    )
    tables = dft_tables(side)

    def one_wave(inputs):
        return blur_wave(inputs[0], inputs[1], mixing, tables)

    blurred, up, down = lax.map(one_wave, (scene, extended))
    from_above = from_behind(down, "tile", 1)
    from_below = from_behind(up, "tile", -1)
    blurred = (
        blurred
        + jnp.pad(from_above, ((0, 0), (0, strip - margin), (0, 0)))
        + jnp.pad(from_below, ((0, 0), (strip - margin, 0), (0, 0)))
    )
    groups = lax.axis_size("wave")
    width = blurred.shape[-1]
    pieces = blurred.reshape(wave_count, groups, strip // groups, width)
    gathered = lax.all_to_all(pieces, "wave", 1, 1, tiled=True)
    channels = response.shape[0]
    spectral = response.reshape(channels, groups, wave_count)
    colour = jnp.einsum("csi,isrx->crx", spectral, gathered, precision=highest)
    return colour


def solution(mesh):
    in_specs = (
        P("wave", "tile", None),
        P("wave", "tile", None, None, None),
        P("tile", None, None),
        P("tile", None, None),
        P(),
    )
    out_specs = P(None, ("tile", "wave"), None)
    return jax.shard_map(
        per_device, mesh=mesh, in_specs=in_specs, out_specs=out_specs, check_vma=False
    )
```

```python
import math

import jax
import jax.numpy as jnp
from jax import lax
from jax.sharding import PartitionSpec as P


highest = lax.Precision.HIGHEST
high = lax.Precision.HIGH


def with_halo(cells, sides, width):
    for axis, dim in sides:
        count = lax.axis_size(axis)
        ends = count - 1
        head = lax.slice_in_dim(cells, 0, width, axis=dim)
        tail = lax.slice_in_dim(cells, cells.shape[dim] - width, cells.shape[dim], axis=dim)
        cells = jnp.concatenate(
            [
                lax.ppermute(tail, axis, [(i, (i + 1) % count) for i in range(ends)]),
                cells,
                lax.ppermute(head, axis, [((i + 1) % count, i) for i in range(ends)]),
            ],
            axis=dim,
        )
    return cells


def from_behind(shard, axis, by):
    size = lax.axis_size(axis)
    pairs = [(i, i + by) for i in range(size) if 0 <= i + by < size]
    return lax.ppermute(shard, axis, pairs)


def angle_table(rows, cols, length):
    products = lax.iota(jnp.int32, rows)[:, None] * lax.iota(jnp.int32, cols)[None, :] % length
    angles = products.astype(jnp.float32) * (2.0 * math.pi / length)
    return jnp.cos(angles), jnp.sin(angles)


def dft_tables(side):
    length = 2 * side
    cos_full, sin_full = angle_table(length, length, length)
    first_row = (lax.iota(jnp.int32, side) == 0)
    signs = jnp.where(lax.iota(jnp.int32, length) % 2 == 0, 1.0, -1.0).astype(jnp.float32)
    cos_in, sin_in = cos_full[:side, :side], sin_full[:side, :side]
    first = jnp.stack([cos_in, jnp.where(first_row[None, :], signs[:side, None], -sin_in)], axis=1)
    cos_k, sin_k = cos_full[:, :side], sin_full[:, :side]
    rows_fwd = jnp.stack(
        [jnp.stack([cos_k, sin_k], axis=1), jnp.stack([-sin_k, cos_k], axis=1)], axis=0
    ).reshape(2 * length, 2, side)
    rows_inv = jnp.concatenate(
        [
            jnp.concatenate([cos_full, -sin_full], axis=1),
            jnp.concatenate([sin_full, cos_full], axis=1),
        ],
        axis=0,
    )
    cos_out = jnp.where(first_row[:, None], 1.0, 2.0 * cos_full[:side])
    sin_out = jnp.where(first_row[:, None], signs[None, :], -2.0 * sin_full[:side])
    last = jnp.stack([cos_out, sin_out], axis=0) / float(length * length)
    return first, rows_fwd, rows_inv, last


def forward(blocks, first, rows_fwd):
    side = blocks.shape[1]
    length = rows_fwd.shape[0] // 2
    packed = jnp.einsum("tab,bpl->tpla", blocks, first, precision=highest)
    rows_fwd = rows_fwd.reshape(2 * length, 2, side)
    spec = jnp.einsum("tpla,opa->tlo", packed, rows_fwd, precision=highest)
    return spec[..., :length], spec[..., length:]


def reverse(values):
    return jnp.roll(jnp.flip(values, axis=-1), 1, axis=-1)


def split_packed(real, imag):
    real_rev, imag_rev = reverse(real), reverse(imag)
    low = (0.5 * (real + real_rev), 0.5 * (imag - imag_rev))
    top = (0.5 * (imag + imag_rev), -0.5 * (real - real_rev))
    return low, top


def times(a, b):
    return (a[0] * b[0] - a[1] * b[1], a[0] * b[1] + a[1] * b[0])


def product(scene_spec, psf_spec):
    prod_real, prod_imag = times(scene_spec, psf_spec)
    scene_low, scene_top = split_packed(scene_spec[0][:, 0], scene_spec[1][:, 0])
    psf_low, psf_top = split_packed(psf_spec[0][:, 0], psf_spec[1][:, 0])
    low = times(scene_low, psf_low)
    top = times(scene_top, psf_top)
    first_column = (lax.iota(jnp.int32, prod_real.shape[1]) == 0)[:, None]
    prod_real = jnp.where(first_column, (low[0] - top[1])[:, None, :], prod_real)
    prod_imag = jnp.where(first_column, (low[1] + top[0])[:, None, :], prod_imag)
    return prod_real, prod_imag


def inverse(prod_real, prod_imag, rows_inv, last):
    tiles, half, length = prod_real.shape
    stacked = jnp.concatenate([prod_real, prod_imag], axis=-1)
    both = jnp.einsum("tlq,oq->tol", stacked, rows_inv, precision=high)
    both = both.reshape(tiles, 2, length, half)
    return jnp.einsum("tpml,pln->tmn", both, last, precision=high)


def blur_wave(scene_plane, extended_plane, mixing, tables):
    first, rows_fwd, rows_inv, last = tables
    slots, tile_cols, side = (
        extended_plane.shape[0] * extended_plane.shape[1],
        extended_plane.shape[1],
        extended_plane.shape[-1],
    )
    tile_rows = extended_plane.shape[0] - 2
    tiles = tile_rows * tile_cols
    width = scene_plane.shape[1]
    margin = side // 2
    psf_set = jnp.dot(mixing, extended_plane.reshape(slots, side * side), precision=highest)
    psf_set = psf_set.reshape(tiles, side, side)
    tile_set = (
        scene_plane.reshape(tile_rows, side, tile_cols, side)
        .transpose(0, 2, 1, 3)
        .reshape(tiles, side, side)
    )
    spec_real, spec_imag = forward(jnp.concatenate([tile_set, psf_set]), first, rows_fwd)
    prod_real, prod_imag = product(
        (spec_real[:tiles], spec_imag[:tiles]), (spec_real[tiles:], spec_imag[tiles:])
    )
    circular = inverse(prod_real, prod_imag, rows_inv, last)
    circular = circular.reshape(tile_rows, tile_cols, 2 * side, 2 * side)
    left_half = jnp.pad(circular[..., :side], ((0, 0), (0, 1), (0, 0), (0, 0)))
    right_half = jnp.pad(circular[..., side:], ((0, 0), (1, 0), (0, 0), (0, 0)))
    columns = (left_half + right_half).transpose(0, 2, 1, 3)
    columns = columns.reshape(tile_rows, 2 * side, (tile_cols + 1) * side)
    columns = columns[:, :, margin : margin + tile_cols * side]
    top_half = jnp.pad(columns[:, :side], ((0, 1), (0, 0), (0, 0)))
    bottom_half = jnp.pad(columns[:, side:], ((1, 0), (0, 0), (0, 0)))
    return (top_half + bottom_half).reshape((tile_rows + 1) * side, width)


def per_device(scene, bank, psf_index, psf_weight, response):
    wave_count, tile_rows, tile_cols, side = (
        bank.shape[0],
        bank.shape[1],
        bank.shape[2],
        bank.shape[3],
    )
    entries = psf_index.shape[-1]
    margin = side // 2
    strip = tile_rows * side
    extended = with_halo(bank, (("tile", 1),), 1)
    first_slot = (lax.axis_index("tile") * tile_rows - 1) * tile_cols
    local_slot = psf_index.reshape(tile_rows * tile_cols, entries) - first_slot
    slot_ids = lax.iota(jnp.int32, (tile_rows + 2) * tile_cols)
    fraction = psf_weight.reshape(tile_rows * tile_cols, entries).astype(jnp.float32) / 65536.0
    mixing = jnp.sum(
        jnp.where(local_slot[:, :, None] == slot_ids[None, None, :], fraction[:, :, None], 0.0),
        axis=1,
    )
    tables = dft_tables(side)

    def one_wave(inputs):
        return blur_wave(inputs[0], inputs[1], mixing, tables)

    summed = lax.map(one_wave, (scene, extended))
    from_above = from_behind(summed[:, strip + margin :], "tile", 1)
    from_below = from_behind(summed[:, :margin], "tile", -1)
    blurred = summed[:, margin : margin + strip]
    blurred = blurred.at[:, :margin].add(from_above)
    blurred = blurred.at[:, strip - margin :].add(from_below)
    groups = lax.axis_size("wave")
    width = blurred.shape[-1]
    pieces = blurred.reshape(wave_count, groups, strip // groups, width)
    inner = 4 if groups % 4 == 0 else 1
    outer = groups // inner
    own = lax.axis_index("wave")
    own_outer, own_inner = own // inner, own % inner
    received, sources = [], []
    for step_outer in range(outer):
        for step_inner in range(inner):
            target = ((own_outer + step_outer) % outer) * inner + (own_inner + step_inner) % inner
            chunk = lax.dynamic_index_in_dim(pieces, target, axis=1, keepdims=False)
            if step_outer or step_inner:
                pairs = [
                    (o * inner + i, ((o + step_outer) % outer) * inner + (i + step_inner) % inner)
                    for o in range(outer)
                    for i in range(inner)
                ]
                chunk = lax.ppermute(chunk, "wave", pairs)
            received.append(chunk)
            sources.append(
                ((own_outer - step_outer) % outer) * inner + (own_inner - step_inner) % inner
            )
    gathered = jnp.stack(received, axis=1)
    channels = response.shape[0]
    spectral = response.reshape(channels, groups, wave_count)[:, jnp.stack(sources)]
    colour = jnp.einsum("csi,isrx->crx", spectral, gathered, precision=highest)
    return colour


def solution(mesh):
    in_specs = (
        P("wave", "tile", None),
        P("wave", "tile", None, None, None),
        P("tile", None, None),
        P("tile", None, None),
        P(),
    )
    out_specs = P(None, ("tile", "wave"), None)
    return jax.shard_map(
        per_device, mesh=mesh, in_specs=in_specs, out_specs=out_specs, check_vma=False
    )
```

```python
import math

import jax
import jax.numpy as jnp
from jax import lax
from jax.sharding import PartitionSpec as P


highest = lax.Precision.HIGHEST
high = lax.Precision.HIGH


def with_halo(cells, sides, width):
    for axis, dim in sides:
        count = lax.axis_size(axis)
        ends = count - 1
        head = lax.slice_in_dim(cells, 0, width, axis=dim)
        tail = lax.slice_in_dim(cells, cells.shape[dim] - width, cells.shape[dim], axis=dim)
        cells = jnp.concatenate(
            [
                lax.ppermute(tail, axis, [(i, (i + 1) % count) for i in range(ends)]),
                cells,
                lax.ppermute(head, axis, [((i + 1) % count, i) for i in range(ends)]),
            ],
            axis=dim,
        )
    return cells


def from_behind(shard, axis, by):
    size = lax.axis_size(axis)
    pairs = [(i, i + by) for i in range(size) if 0 <= i + by < size]
    return lax.ppermute(shard, axis, pairs)


def angle_table(rows, cols, length):
    products = lax.iota(jnp.int32, rows)[:, None] * lax.iota(jnp.int32, cols)[None, :] % length
    angles = products.astype(jnp.float32) * (2.0 * math.pi / length)
    return jnp.cos(angles), jnp.sin(angles)


def dft_tables(side):
    length = 2 * side
    cos_full, sin_full = angle_table(length, length, length)
    first_row = (lax.iota(jnp.int32, side) == 0)
    signs = jnp.where(lax.iota(jnp.int32, length) % 2 == 0, 1.0, -1.0).astype(jnp.float32)
    cos_in, sin_in = cos_full[:side, :side], sin_full[:side, :side]
    first = jnp.stack([cos_in, jnp.where(first_row[None, :], signs[:side, None], -sin_in)], axis=1)
    cos_k, sin_k = cos_full[:, :side], sin_full[:, :side]
    rows_fwd = jnp.stack(
        [jnp.stack([cos_k, sin_k], axis=1), jnp.stack([-sin_k, cos_k], axis=1)], axis=0
    ).reshape(2 * length, 2, side)
    rows_inv = jnp.concatenate(
        [
            jnp.concatenate([cos_full, -sin_full], axis=1),
            jnp.concatenate([sin_full, cos_full], axis=1),
        ],
        axis=0,
    )
    cos_out = jnp.where(first_row[:, None], 1.0, 2.0 * cos_full[:side])
    sin_out = jnp.where(first_row[:, None], signs[None, :], -2.0 * sin_full[:side])
    last = jnp.stack([cos_out, sin_out], axis=0) / float(length * length)
    return first, rows_fwd, rows_inv, last


def forward(blocks, first, rows_fwd):
    side = blocks.shape[1]
    length = rows_fwd.shape[0] // 2
    packed = jnp.einsum("tab,bpl->tpla", blocks, first, precision=highest)
    rows_fwd = rows_fwd.reshape(2 * length, 2, side)
    spec = jnp.einsum("tpla,opa->tlo", packed, rows_fwd, precision=highest)
    return spec[..., :length], spec[..., length:]


def reverse(values):
    return jnp.roll(jnp.flip(values, axis=-1), 1, axis=-1)


def split_packed(real, imag):
    real_rev, imag_rev = reverse(real), reverse(imag)
    low = (0.5 * (real + real_rev), 0.5 * (imag - imag_rev))
    top = (0.5 * (imag + imag_rev), -0.5 * (real - real_rev))
    return low, top


def times(a, b):
    return (a[0] * b[0] - a[1] * b[1], a[0] * b[1] + a[1] * b[0])


def product(scene_spec, psf_spec):
    prod_real, prod_imag = times(scene_spec, psf_spec)
    scene_low, scene_top = split_packed(scene_spec[0][:, 0], scene_spec[1][:, 0])
    psf_low, psf_top = split_packed(psf_spec[0][:, 0], psf_spec[1][:, 0])
    low = times(scene_low, psf_low)
    top = times(scene_top, psf_top)
    first_column = (lax.iota(jnp.int32, prod_real.shape[1]) == 0)[:, None]
    prod_real = jnp.where(first_column, (low[0] - top[1])[:, None, :], prod_real)
    prod_imag = jnp.where(first_column, (low[1] + top[0])[:, None, :], prod_imag)
    return prod_real, prod_imag


def split_bf16(values):
    upper = values.astype(jnp.bfloat16)
    return upper, (values - upper.astype(jnp.float32)).astype(jnp.bfloat16)


def three_pass(spec, data, table):
    data_hi, data_lo = split_bf16(data)
    table_hi, table_lo = split_bf16(table)
    terms = [(data_hi, table_hi), (data_lo, table_hi), (data_hi, table_lo)]
    return sum(jnp.einsum(spec, a, b, preferred_element_type=jnp.float32) for a, b in terms)


def inverse(prod_real, prod_imag, rows_inv, last):
    tiles, half, length = prod_real.shape
    stacked = jnp.concatenate([prod_real, prod_imag], axis=-1)
    both = three_pass("tlq,oq->tol", stacked, rows_inv)
    both = both.reshape(tiles, 2, length, half)
    return jnp.einsum("tpml,pln->tmn", both, last, precision=high)


def blur_wave(scene_plane, extended_plane, mixing, tables):
    first, rows_fwd, rows_inv, last = tables
    slots, tile_cols, side = (
        extended_plane.shape[0] * extended_plane.shape[1],
        extended_plane.shape[1],
        extended_plane.shape[-1],
    )
    tile_rows = extended_plane.shape[0] - 2
    tiles = tile_rows * tile_cols
    width = scene_plane.shape[1]
    margin = side // 2
    psf_set = jnp.dot(mixing, extended_plane.reshape(slots, side * side), precision=highest)
    psf_set = psf_set.reshape(tiles, side, side)
    tile_set = (
        scene_plane.reshape(tile_rows, side, tile_cols, side)
        .transpose(0, 2, 1, 3)
        .reshape(tiles, side, side)
    )
    spec_real, spec_imag = forward(jnp.concatenate([tile_set, psf_set]), first, rows_fwd)
    prod_real, prod_imag = product(
        (spec_real[:tiles], spec_imag[:tiles]), (spec_real[tiles:], spec_imag[tiles:])
    )
    circular = inverse(prod_real, prod_imag, rows_inv, last)
    circular = circular.reshape(tile_rows, tile_cols, 2 * side, 2 * side)
    left_half = jnp.pad(circular[..., :side], ((0, 0), (0, 1), (0, 0), (0, 0)))
    right_half = jnp.pad(circular[..., side:], ((0, 0), (1, 0), (0, 0), (0, 0)))
    columns = (left_half + right_half).transpose(0, 2, 1, 3)
    columns = columns.reshape(tile_rows, 2 * side, (tile_cols + 1) * side)
    columns = columns[:, :, margin : margin + tile_cols * side]
    top_half = jnp.pad(columns[:, :side], ((0, 1), (0, 0), (0, 0)))
    bottom_half = jnp.pad(columns[:, side:], ((1, 0), (0, 0), (0, 0)))
    return (top_half + bottom_half).reshape((tile_rows + 1) * side, width)


def per_device(scene, bank, psf_index, psf_weight, response):
    wave_count, tile_rows, tile_cols, side = (
        bank.shape[0],
        bank.shape[1],
        bank.shape[2],
        bank.shape[3],
    )
    entries = psf_index.shape[-1]
    margin = side // 2
    strip = tile_rows * side
    extended = with_halo(bank, (("tile", 1),), 1)
    first_slot = (lax.axis_index("tile") * tile_rows - 1) * tile_cols
    local_slot = psf_index.reshape(tile_rows * tile_cols, entries) - first_slot
    slot_ids = lax.iota(jnp.int32, (tile_rows + 2) * tile_cols)
    fraction = psf_weight.reshape(tile_rows * tile_cols, entries).astype(jnp.float32) / 65536.0
    mixing = jnp.sum(
        jnp.where(local_slot[:, :, None] == slot_ids[None, None, :], fraction[:, :, None], 0.0),
        axis=1,
    )
    tables = dft_tables(side)

    def one_wave(inputs):
        return blur_wave(inputs[0], inputs[1], mixing, tables)

    summed = lax.map(one_wave, (scene, extended))
    from_above = from_behind(summed[:, strip + margin :], "tile", 1)
    from_below = from_behind(summed[:, :margin], "tile", -1)
    blurred = summed[:, margin : margin + strip]
    blurred = blurred.at[:, :margin].add(from_above)
    blurred = blurred.at[:, strip - margin :].add(from_below)
    groups = lax.axis_size("wave")
    width = blurred.shape[-1]
    pieces = blurred.reshape(wave_count, groups, strip // groups, width)
    gathered = lax.all_to_all(pieces, "wave", 1, 1, tiled=True)
    channels = response.shape[0]
    spectral = response.reshape(channels, groups, wave_count)
    colour = jnp.einsum("csi,isrx->crx", spectral, gathered, precision=highest)
    return colour


def solution(mesh):
    in_specs = (
        P("wave", "tile", None),
        P("wave", "tile", None, None, None),
        P("tile", None, None),
        P("tile", None, None),
        P(),
    )
    out_specs = P(None, ("tile", "wave"), None)
    return jax.shard_map(
        per_device, mesh=mesh, in_specs=in_specs, out_specs=out_specs, check_vma=False
    )
```

```python
import math

import jax
import jax.numpy as jnp
from jax import lax
from jax.sharding import PartitionSpec as P


highest = lax.Precision.HIGHEST
high = lax.Precision.HIGH


def with_halo(cells, sides, width):
    for axis, dim in sides:
        count = lax.axis_size(axis)
        ends = count - 1
        head = lax.slice_in_dim(cells, 0, width, axis=dim)
        tail = lax.slice_in_dim(cells, cells.shape[dim] - width, cells.shape[dim], axis=dim)
        cells = jnp.concatenate(
            [
                lax.ppermute(tail, axis, [(i, (i + 1) % count) for i in range(ends)]),
                cells,
                lax.ppermute(head, axis, [((i + 1) % count, i) for i in range(ends)]),
            ],
            axis=dim,
        )
    return cells


def from_behind(shard, axis, by):
    size = lax.axis_size(axis)
    pairs = [(i, i + by) for i in range(size) if 0 <= i + by < size]
    return lax.ppermute(shard, axis, pairs)


def angle_table(rows, cols, length):
    products = lax.iota(jnp.int32, rows)[:, None] * lax.iota(jnp.int32, cols)[None, :] % length
    angles = products.astype(jnp.float32) * (2.0 * math.pi / length)
    return jnp.cos(angles), jnp.sin(angles)


def dft_tables(side):
    length = 2 * side
    cos_full, sin_full = angle_table(length, length, length)
    first_row = (lax.iota(jnp.int32, side) == 0)
    signs = jnp.where(lax.iota(jnp.int32, length) % 2 == 0, 1.0, -1.0).astype(jnp.float32)
    cos_in, sin_in = cos_full[:side, :side], sin_full[:side, :side]
    first = jnp.stack([cos_in, jnp.where(first_row[None, :], signs[:side, None], -sin_in)], axis=1)
    cos_k, sin_k = cos_full[:, :side], sin_full[:, :side]
    rows_fwd = jnp.stack(
        [jnp.stack([cos_k, sin_k], axis=1), jnp.stack([-sin_k, cos_k], axis=1)], axis=0
    ).reshape(2 * length, 2, side)
    rows_inv = jnp.concatenate(
        [
            jnp.concatenate([cos_full, -sin_full], axis=1),
            jnp.concatenate([sin_full, cos_full], axis=1),
        ],
        axis=0,
    )
    cos_out = jnp.where(first_row[:, None], 1.0, 2.0 * cos_full[:side])
    sin_out = jnp.where(first_row[:, None], signs[None, :], -2.0 * sin_full[:side])
    last = jnp.stack([cos_out, sin_out], axis=0) / float(length * length)
    return first, rows_fwd, rows_inv, last


def split_three(values):
    upper = values.astype(jnp.bfloat16)
    rest = values - upper.astype(jnp.float32)
    middle = rest.astype(jnp.bfloat16)
    return upper, middle, (rest - middle.astype(jnp.float32)).astype(jnp.bfloat16)


def six_terms(spec, data, table):
    data_parts = split_three(data)
    table_parts = split_three(table)
    pairs = [(0, 0), (1, 0), (2, 0), (0, 1), (1, 1), (0, 2)]
    stacked_data = jnp.concatenate([data_parts[d] for d, _ in pairs], axis=-1)
    stacked_table = jnp.concatenate([table_parts[t] for _, t in pairs], axis=0)
    return jnp.einsum(spec, stacked_data, stacked_table, preferred_element_type=jnp.float32)


def forward(blocks, first, rows_fwd):
    side = blocks.shape[1]
    length = rows_fwd.shape[0] // 2
    packed = six_terms("tab,bpl->tpla", blocks, first)
    rows_fwd = rows_fwd.reshape(2 * length, 2, side)
    spec = jnp.einsum("tpla,opa->tlo", packed, rows_fwd, precision=highest)
    return spec[..., :length], spec[..., length:]


def reverse(values):
    return jnp.roll(jnp.flip(values, axis=-1), 1, axis=-1)


def split_packed(real, imag):
    real_rev, imag_rev = reverse(real), reverse(imag)
    low = (0.5 * (real + real_rev), 0.5 * (imag - imag_rev))
    top = (0.5 * (imag + imag_rev), -0.5 * (real - real_rev))
    return low, top


def times(a, b):
    return (a[0] * b[0] - a[1] * b[1], a[0] * b[1] + a[1] * b[0])


def product(scene_spec, psf_spec):
    prod_real, prod_imag = times(scene_spec, psf_spec)
    scene_low, scene_top = split_packed(scene_spec[0][:, 0], scene_spec[1][:, 0])
    psf_low, psf_top = split_packed(psf_spec[0][:, 0], psf_spec[1][:, 0])
    low = times(scene_low, psf_low)
    top = times(scene_top, psf_top)
    first_column = (lax.iota(jnp.int32, prod_real.shape[1]) == 0)[:, None]
    prod_real = jnp.where(first_column, (low[0] - top[1])[:, None, :], prod_real)
    prod_imag = jnp.where(first_column, (low[1] + top[0])[:, None, :], prod_imag)
    return prod_real, prod_imag


def split_bf16(values):
    upper = values.astype(jnp.bfloat16)
    return upper, (values - upper.astype(jnp.float32)).astype(jnp.bfloat16)


def three_pass(spec, data, table):
    data_hi, data_lo = split_bf16(data)
    table_hi, table_lo = split_bf16(table)
    terms = [(data_hi, table_hi), (data_lo, table_hi), (data_hi, table_lo)]
    return sum(jnp.einsum(spec, a, b, preferred_element_type=jnp.float32) for a, b in terms)


def inverse(prod_real, prod_imag, rows_inv, last):
    tiles, half, length = prod_real.shape
    stacked = jnp.concatenate([prod_real, prod_imag], axis=-1)
    both = three_pass("tlq,oq->tol", stacked, rows_inv)
    both = both.reshape(tiles, 2, length, half)
    return jnp.einsum("tpml,pln->tmn", both, last, precision=high)


def blur_wave(scene_plane, extended_plane, mixing, tables):
    first, rows_fwd, rows_inv, last = tables
    slots, tile_cols, side = (
        extended_plane.shape[0] * extended_plane.shape[1],
        extended_plane.shape[1],
        extended_plane.shape[-1],
    )
    tile_rows = extended_plane.shape[0] - 2
    tiles = tile_rows * tile_cols
    width = scene_plane.shape[1]
    margin = side // 2
    psf_set = jnp.dot(mixing, extended_plane.reshape(slots, side * side), precision=highest)
    psf_set = psf_set.reshape(tiles, side, side)
    tile_set = (
        scene_plane.reshape(tile_rows, side, tile_cols, side)
        .transpose(0, 2, 1, 3)
        .reshape(tiles, side, side)
    )
    spec_real, spec_imag = forward(jnp.concatenate([tile_set, psf_set]), first, rows_fwd)
    prod_real, prod_imag = product(
        (spec_real[:tiles], spec_imag[:tiles]), (spec_real[tiles:], spec_imag[tiles:])
    )
    circular = inverse(prod_real, prod_imag, rows_inv, last)
    circular = circular.reshape(tile_rows, tile_cols, 2 * side, 2 * side)
    left_half = jnp.pad(circular[..., :side], ((0, 0), (0, 1), (0, 0), (0, 0)))
    right_half = jnp.pad(circular[..., side:], ((0, 0), (1, 0), (0, 0), (0, 0)))
    columns = (left_half + right_half).transpose(0, 2, 1, 3)
    columns = columns.reshape(tile_rows, 2 * side, (tile_cols + 1) * side)
    columns = columns[:, :, margin : margin + tile_cols * side]
    top_half = jnp.pad(columns[:, :side], ((0, 1), (0, 0), (0, 0)))
    bottom_half = jnp.pad(columns[:, side:], ((1, 0), (0, 0), (0, 0)))
    return (top_half + bottom_half).reshape((tile_rows + 1) * side, width)


def per_device(scene, bank, psf_index, psf_weight, response):
    wave_count, tile_rows, tile_cols, side = (
        bank.shape[0],
        bank.shape[1],
        bank.shape[2],
        bank.shape[3],
    )
    entries = psf_index.shape[-1]
    margin = side // 2
    strip = tile_rows * side
    extended = with_halo(bank, (("tile", 1),), 1)
    first_slot = (lax.axis_index("tile") * tile_rows - 1) * tile_cols
    local_slot = psf_index.reshape(tile_rows * tile_cols, entries) - first_slot
    slot_ids = lax.iota(jnp.int32, (tile_rows + 2) * tile_cols)
    fraction = psf_weight.reshape(tile_rows * tile_cols, entries).astype(jnp.float32) / 65536.0
    mixing = jnp.sum(
        jnp.where(local_slot[:, :, None] == slot_ids[None, None, :], fraction[:, :, None], 0.0),
        axis=1,
    )
    tables = dft_tables(side)

    def one_wave(inputs):
        return blur_wave(inputs[0], inputs[1], mixing, tables)

    summed = lax.map(one_wave, (scene, extended))
    from_above = from_behind(summed[:, strip + margin :], "tile", 1)
    from_below = from_behind(summed[:, :margin], "tile", -1)
    blurred = summed[:, margin : margin + strip]
    blurred = blurred.at[:, :margin].add(from_above)
    blurred = blurred.at[:, strip - margin :].add(from_below)
    groups = lax.axis_size("wave")
    width = blurred.shape[-1]
    pieces = blurred.reshape(wave_count, groups, strip // groups, width)
    gathered = lax.all_to_all(pieces, "wave", 1, 1, tiled=True)
    channels = response.shape[0]
    spectral = response.reshape(channels, groups, wave_count)
    colour = jnp.einsum("csi,isrx->crx", spectral, gathered, precision=highest)
    return colour


def solution(mesh):
    in_specs = (
        P("wave", "tile", None),
        P("wave", "tile", None, None, None),
        P("tile", None, None),
        P("tile", None, None),
        P(),
    )
    out_specs = P(None, ("tile", "wave"), None)
    return jax.shard_map(
        per_device, mesh=mesh, in_specs=in_specs, out_specs=out_specs, check_vma=False
    )
```

```python
import math

import jax
import jax.numpy as jnp
from jax import lax
from jax.sharding import PartitionSpec as P


highest = lax.Precision.HIGHEST
high = lax.Precision.HIGH


def with_halo(cells, sides, width):
    for axis, dim in sides:
        count = lax.axis_size(axis)
        ends = count - 1
        head = lax.slice_in_dim(cells, 0, width, axis=dim)
        tail = lax.slice_in_dim(cells, cells.shape[dim] - width, cells.shape[dim], axis=dim)
        cells = jnp.concatenate(
            [
                lax.ppermute(tail, axis, [(i, (i + 1) % count) for i in range(ends)]),
                cells,
                lax.ppermute(head, axis, [((i + 1) % count, i) for i in range(ends)]),
            ],
            axis=dim,
        )
    return cells


def from_behind(shard, axis, by):
    size = lax.axis_size(axis)
    pairs = [(i, i + by) for i in range(size) if 0 <= i + by < size]
    return lax.ppermute(shard, axis, pairs)


def angle_table(rows, cols, length):
    products = lax.iota(jnp.int32, rows)[:, None] * lax.iota(jnp.int32, cols)[None, :] % length
    angles = products.astype(jnp.float32) * (2.0 * math.pi / length)
    return jnp.cos(angles), jnp.sin(angles)


def dft_tables(side):
    length = 2 * side
    cos_full, sin_full = angle_table(length, length, length)
    first_row = (lax.iota(jnp.int32, side) == 0)
    signs = jnp.where(lax.iota(jnp.int32, length) % 2 == 0, 1.0, -1.0).astype(jnp.float32)
    cos_in, sin_in = cos_full[:side, :side], sin_full[:side, :side]
    first = jnp.stack([cos_in, jnp.where(first_row[None, :], signs[:side, None], -sin_in)], axis=1)
    cos_k, sin_k = cos_full[:, :side], sin_full[:, :side]
    rows_fwd = jnp.stack(
        [jnp.stack([cos_k, sin_k], axis=1), jnp.stack([-sin_k, cos_k], axis=1)], axis=0
    ).reshape(2 * length, 2, side)
    rows_inv = jnp.concatenate(
        [
            jnp.concatenate([cos_full, -sin_full], axis=1),
            jnp.concatenate([sin_full, cos_full], axis=1),
        ],
        axis=0,
    )
    cos_out = jnp.where(first_row[:, None], 1.0, 2.0 * cos_full[:side])
    sin_out = jnp.where(first_row[:, None], signs[None, :], -2.0 * sin_full[:side])
    last = jnp.stack([cos_out, sin_out], axis=0) / float(length * length)
    return first, rows_fwd, rows_inv, last


def forward(blocks, first, rows_fwd):
    side = blocks.shape[1]
    length = rows_fwd.shape[0] // 2
    packed = jnp.einsum("tab,bpl->tpla", blocks, first, precision=highest)
    rows_fwd = rows_fwd.reshape(2 * length, 2, side)
    spec = jnp.einsum("tpla,opa->tlo", packed, rows_fwd, precision=highest)
    return spec[..., :length], spec[..., length:]


def reverse(values):
    return jnp.roll(jnp.flip(values, axis=-1), 1, axis=-1)


def split_packed(real, imag):
    real_rev, imag_rev = reverse(real), reverse(imag)
    low = (0.5 * (real + real_rev), 0.5 * (imag - imag_rev))
    top = (0.5 * (imag + imag_rev), -0.5 * (real - real_rev))
    return low, top


def times(a, b):
    return (a[0] * b[0] - a[1] * b[1], a[0] * b[1] + a[1] * b[0])


def product(scene_spec, psf_spec):
    prod_real, prod_imag = times(scene_spec, psf_spec)
    scene_low, scene_top = split_packed(scene_spec[0][:, 0], scene_spec[1][:, 0])
    psf_low, psf_top = split_packed(psf_spec[0][:, 0], psf_spec[1][:, 0])
    low = times(scene_low, psf_low)
    top = times(scene_top, psf_top)
    first_column = (lax.iota(jnp.int32, prod_real.shape[1]) == 0)[:, None]
    prod_real = jnp.where(first_column, (low[0] - top[1])[:, None, :], prod_real)
    prod_imag = jnp.where(first_column, (low[1] + top[0])[:, None, :], prod_imag)
    return prod_real, prod_imag


def split_bf16(values):
    upper = values.astype(jnp.bfloat16)
    return upper, (values - upper.astype(jnp.float32)).astype(jnp.bfloat16)


def three_pass(spec, data, table):
    data_hi, data_lo = split_bf16(data)
    table_hi, table_lo = split_bf16(table)
    terms = [(data_hi, table_hi), (data_lo, table_hi), (data_hi, table_lo)]
    return sum(jnp.einsum(spec, a, b, preferred_element_type=jnp.float32) for a, b in terms)


def inverse(prod_real, prod_imag, rows_inv, last):
    tiles, half, length = prod_real.shape
    stacked = jnp.concatenate([prod_real, prod_imag], axis=-1)
    both = three_pass("tlq,oq->tol", stacked, rows_inv)
    both = both.reshape(tiles, 2, length, half)
    return three_pass("tpml,pln->tmn", both, last)


def blur_wave(scene_plane, extended_plane, mixing, tables):
    first, rows_fwd, rows_inv, last = tables
    slots, tile_cols, side = (
        extended_plane.shape[0] * extended_plane.shape[1],
        extended_plane.shape[1],
        extended_plane.shape[-1],
    )
    tile_rows = extended_plane.shape[0] - 2
    tiles = tile_rows * tile_cols
    width = scene_plane.shape[1]
    margin = side // 2
    psf_set = jnp.dot(mixing, extended_plane.reshape(slots, side * side), precision=highest)
    psf_set = psf_set.reshape(tiles, side, side)
    tile_set = (
        scene_plane.reshape(tile_rows, side, tile_cols, side)
        .transpose(0, 2, 1, 3)
        .reshape(tiles, side, side)
    )
    spec_real, spec_imag = forward(jnp.concatenate([tile_set, psf_set]), first, rows_fwd)
    prod_real, prod_imag = product(
        (spec_real[:tiles], spec_imag[:tiles]), (spec_real[tiles:], spec_imag[tiles:])
    )
    circular = inverse(prod_real, prod_imag, rows_inv, last)
    circular = circular.reshape(tile_rows, tile_cols, 2 * side, 2 * side)
    left_half = jnp.pad(circular[..., :side], ((0, 0), (0, 1), (0, 0), (0, 0)))
    right_half = jnp.pad(circular[..., side:], ((0, 0), (1, 0), (0, 0), (0, 0)))
    columns = (left_half + right_half).transpose(0, 2, 1, 3)
    columns = columns.reshape(tile_rows, 2 * side, (tile_cols + 1) * side)
    columns = columns[:, :, margin : margin + tile_cols * side]
    top_half = jnp.pad(columns[:, :side], ((0, 1), (0, 0), (0, 0)))
    bottom_half = jnp.pad(columns[:, side:], ((1, 0), (0, 0), (0, 0)))
    return (top_half + bottom_half).reshape((tile_rows + 1) * side, width)


def per_device(scene, bank, psf_index, psf_weight, response):
    wave_count, tile_rows, tile_cols, side = (
        bank.shape[0],
        bank.shape[1],
        bank.shape[2],
        bank.shape[3],
    )
    entries = psf_index.shape[-1]
    margin = side // 2
    strip = tile_rows * side
    extended = with_halo(bank, (("tile", 1),), 1)
    first_slot = (lax.axis_index("tile") * tile_rows - 1) * tile_cols
    local_slot = psf_index.reshape(tile_rows * tile_cols, entries) - first_slot
    slot_ids = lax.iota(jnp.int32, (tile_rows + 2) * tile_cols)
    fraction = psf_weight.reshape(tile_rows * tile_cols, entries).astype(jnp.float32) / 65536.0
    mixing = jnp.sum(
        jnp.where(local_slot[:, :, None] == slot_ids[None, None, :], fraction[:, :, None], 0.0),
        axis=1,
    )
    tables = dft_tables(side)

    def one_wave(inputs):
        return blur_wave(inputs[0], inputs[1], mixing, tables)

    summed = lax.map(one_wave, (scene, extended))
    from_above = from_behind(summed[:, strip + margin :], "tile", 1)
    from_below = from_behind(summed[:, :margin], "tile", -1)
    blurred = summed[:, margin : margin + strip]
    blurred = blurred.at[:, :margin].add(from_above)
    blurred = blurred.at[:, strip - margin :].add(from_below)
    groups = lax.axis_size("wave")
    width = blurred.shape[-1]
    pieces = blurred.reshape(wave_count, groups, strip // groups, width)
    gathered = lax.all_to_all(pieces, "wave", 1, 1, tiled=True)
    channels = response.shape[0]
    spectral = response.reshape(channels, groups, wave_count)
    colour = jnp.einsum("csi,isrx->crx", spectral, gathered, precision=highest)
    return colour


def solution(mesh):
    in_specs = (
        P("wave", "tile", None),
        P("wave", "tile", None, None, None),
        P("tile", None, None),
        P("tile", None, None),
        P(),
    )
    out_specs = P(None, ("tile", "wave"), None)
    return jax.shard_map(
        per_device, mesh=mesh, in_specs=in_specs, out_specs=out_specs, check_vma=False
    )
```

```python
import math

import jax
import jax.numpy as jnp
from jax import lax
from jax.sharding import PartitionSpec as P


highest = lax.Precision.HIGHEST
high = lax.Precision.HIGH


def with_halo(cells, sides, width):
    for axis, dim in sides:
        count = lax.axis_size(axis)
        ends = count - 1
        head = lax.slice_in_dim(cells, 0, width, axis=dim)
        tail = lax.slice_in_dim(cells, cells.shape[dim] - width, cells.shape[dim], axis=dim)
        cells = jnp.concatenate(
            [
                lax.ppermute(tail, axis, [(i, (i + 1) % count) for i in range(ends)]),
                cells,
                lax.ppermute(head, axis, [((i + 1) % count, i) for i in range(ends)]),
            ],
            axis=dim,
        )
    return cells


def from_behind(shard, axis, by):
    size = lax.axis_size(axis)
    pairs = [(i, i + by) for i in range(size) if 0 <= i + by < size]
    return lax.ppermute(shard, axis, pairs)


def angle_table(rows, cols, length):
    products = lax.iota(jnp.int32, rows)[:, None] * lax.iota(jnp.int32, cols)[None, :] % length
    angles = products.astype(jnp.float32) * (2.0 * math.pi / length)
    return jnp.cos(angles), jnp.sin(angles)


def dft_tables(side):
    length = 2 * side
    cos_full, sin_full = angle_table(length, length, length)
    first_row = (lax.iota(jnp.int32, side) == 0)
    signs = jnp.where(lax.iota(jnp.int32, length) % 2 == 0, 1.0, -1.0).astype(jnp.float32)
    cos_in, sin_in = cos_full[:side, :side], sin_full[:side, :side]
    first = jnp.stack([cos_in, jnp.where(first_row[None, :], signs[:side, None], -sin_in)], axis=1)
    cos_k, sin_k = cos_full[:, :side], sin_full[:, :side]
    rows_fwd = jnp.stack(
        [jnp.stack([cos_k, sin_k], axis=1), jnp.stack([-sin_k, cos_k], axis=1)], axis=0
    ).reshape(2 * length, 2, side)
    rows_inv = jnp.concatenate(
        [
            jnp.concatenate([cos_full, -sin_full], axis=1),
            jnp.concatenate([sin_full, cos_full], axis=1),
        ],
        axis=0,
    )
    cos_out = jnp.where(first_row[:, None], 1.0, 2.0 * cos_full[:side])
    sin_out = jnp.where(first_row[:, None], signs[None, :], -2.0 * sin_full[:side])
    last = jnp.stack([cos_out, sin_out], axis=0) / float(length * length)
    return first, rows_fwd, rows_inv, last


def forward(blocks, first, rows_fwd):
    side = blocks.shape[1]
    length = rows_fwd.shape[0] // 2
    packed = jnp.einsum("tab,bpl->tpla", blocks, first, precision=highest)
    rows_fwd = rows_fwd.reshape(2 * length, 2, side)
    spec = jnp.einsum("tpla,opa->tlo", packed, rows_fwd, precision=highest)
    return spec[..., :length], spec[..., length:]


def reverse(values):
    return jnp.roll(jnp.flip(values, axis=-1), 1, axis=-1)


def split_packed(real, imag):
    real_rev, imag_rev = reverse(real), reverse(imag)
    low = (0.5 * (real + real_rev), 0.5 * (imag - imag_rev))
    top = (0.5 * (imag + imag_rev), -0.5 * (real - real_rev))
    return low, top


def times(a, b):
    return (a[0] * b[0] - a[1] * b[1], a[0] * b[1] + a[1] * b[0])


def product(scene_spec, psf_spec):
    prod_real, prod_imag = times(scene_spec, psf_spec)
    scene_low, scene_top = split_packed(scene_spec[0][:, 0], scene_spec[1][:, 0])
    psf_low, psf_top = split_packed(psf_spec[0][:, 0], psf_spec[1][:, 0])
    low = times(scene_low, psf_low)
    top = times(scene_top, psf_top)
    first_column = (lax.iota(jnp.int32, prod_real.shape[1]) == 0)[:, None]
    prod_real = jnp.where(first_column, (low[0] - top[1])[:, None, :], prod_real)
    prod_imag = jnp.where(first_column, (low[1] + top[0])[:, None, :], prod_imag)
    return prod_real, prod_imag


def split_bf16(values):
    upper = values.astype(jnp.bfloat16)
    return upper, (values - upper.astype(jnp.float32)).astype(jnp.bfloat16)


def three_pass(spec, data, table):
    data_hi, data_lo = split_bf16(data)
    table_hi, table_lo = split_bf16(table)
    terms = [(data_hi, table_hi), (data_lo, table_hi), (data_hi, table_lo)]
    return sum(jnp.einsum(spec, a, b, preferred_element_type=jnp.float32) for a, b in terms)


def inverse(prod_real, prod_imag, rows_inv, last):
    tiles, half, length = prod_real.shape
    stacked = jnp.concatenate([prod_real, prod_imag], axis=-1)
    both = three_pass("tlq,oq->tol", stacked, rows_inv)
    both = both.reshape(tiles, 2, length, half)
    return three_pass("tpml,pln->tmn", both, last)


def blur_wave(scene_plane, extended_plane, mixing, tables):
    first, rows_fwd, rows_inv, last = tables
    slots, tile_cols, side = (
        extended_plane.shape[0] * extended_plane.shape[1],
        extended_plane.shape[1],
        extended_plane.shape[-1],
    )
    tile_rows = extended_plane.shape[0] - 2
    tiles = tile_rows * tile_cols
    width = scene_plane.shape[1]
    margin = side // 2
    psf_set = jnp.dot(mixing, extended_plane.reshape(slots, side * side), precision=highest)
    psf_set = psf_set.reshape(tiles, side, side)
    tile_set = (
        scene_plane.reshape(tile_rows, side, tile_cols, side)
        .transpose(0, 2, 1, 3)
        .reshape(tiles, side, side)
    )
    spec_real, spec_imag = forward(jnp.concatenate([tile_set, psf_set]), first, rows_fwd)
    prod_real, prod_imag = product(
        (spec_real[:tiles], spec_imag[:tiles]), (spec_real[tiles:], spec_imag[tiles:])
    )
    circular = inverse(prod_real, prod_imag, rows_inv, last)
    circular = circular.reshape(tile_rows, tile_cols, 2 * side, 2 * side)
    left_half = jnp.pad(circular[..., :side], ((0, 0), (0, 1), (0, 0), (0, 0)))
    right_half = jnp.pad(circular[..., side:], ((0, 0), (1, 0), (0, 0), (0, 0)))
    columns = (left_half + right_half).transpose(0, 2, 1, 3)
    columns = columns.reshape(tile_rows, 2 * side, (tile_cols + 1) * side)
    columns = columns[:, :, margin : margin + tile_cols * side]
    top_half = jnp.pad(columns[:, :side], ((0, 1), (0, 0), (0, 0)))
    bottom_half = jnp.pad(columns[:, side:], ((1, 0), (0, 0), (0, 0)))
    return (top_half + bottom_half).reshape((tile_rows + 1) * side, width)


def per_device(scene, bank, psf_index, psf_weight, response):
    wave_count, tile_rows, tile_cols, side = (
        bank.shape[0],
        bank.shape[1],
        bank.shape[2],
        bank.shape[3],
    )
    entries = psf_index.shape[-1]
    margin = side // 2
    strip = tile_rows * side
    extended = with_halo(bank, (("tile", 1),), 1)
    first_slot = (lax.axis_index("tile") * tile_rows - 1) * tile_cols
    local_slot = psf_index.reshape(tile_rows * tile_cols, entries) - first_slot
    slot_ids = lax.iota(jnp.int32, (tile_rows + 2) * tile_cols)
    fraction = psf_weight.reshape(tile_rows * tile_cols, entries).astype(jnp.float32) / 65536.0
    mixing = jnp.sum(
        jnp.where(local_slot[:, :, None] == slot_ids[None, None, :], fraction[:, :, None], 0.0),
        axis=1,
    )
    tables = dft_tables(side)

    def one_wave(inputs):
        return blur_wave(inputs[0], inputs[1], mixing, tables)

    summed = lax.map(one_wave, (scene, extended))
    from_above = from_behind(summed[:, strip + margin :], "tile", 1)
    from_below = from_behind(summed[:, :margin], "tile", -1)
    blurred = summed[:, margin : margin + strip]
    blurred = blurred.at[:, :margin].add(from_above)
    blurred = blurred.at[:, strip - margin :].add(from_below)
    groups = lax.axis_size("wave")
    width = blurred.shape[-1]
    pieces = blurred.reshape(wave_count, groups, strip // groups, width)
    gathered = lax.all_to_all(pieces, "wave", 1, 1, tiled=True)
    channels = response.shape[0]
    spectral = response.reshape(channels, groups, wave_count)
    weights = spectral.transpose(0, 2, 1)[:, :, :, None, None]
    colour = jnp.sum(weights * gathered[None], axis=(1, 2))
    return colour


def solution(mesh):
    in_specs = (
        P("wave", "tile", None),
        P("wave", "tile", None, None, None),
        P("tile", None, None),
        P("tile", None, None),
        P(),
    )
    out_specs = P(None, ("tile", "wave"), None)
    return jax.shard_map(
        per_device, mesh=mesh, in_specs=in_specs, out_specs=out_specs, check_vma=False
    )
```
